256 devices in a mesh: row: 32 (over z, x_lo, core), feat: 8 (over y, x_hi).
Axes of the slice: x: 4 (x_hi: 2, x_lo: 2; x = x_hi * 2 + x_lo), y: 4, z: 8, core: 2. Of those that a mesh axis runs over, the one named last changes fastest.
Arguments:
- vectors: bfloat16 [81920, 1024], P('row', 'feat')
- rotation: bfloat16 [1024, 1024], P('feat')
- codes: int32 [81920, 64], P('row', 'feat'), may hold values from 0 to 255
- live_rows: int32 [32], P('row'), may hold values from 640 to 2560
Outputs:
- centroids: float32 [256, 1024], P('row', 'feat')
- grad_t: float32 [1024, 1024], P('row', 'feat')
The draws below stay inside these ranges and needn't reach their ends.
All inputs are finite; a program needn't handle non-finite values.
Results may differ from the reference program's by a relative error of at most 0.00094.
Values may be sent and summed in bfloat16 or wider, within the bound.
No kernel may reach another device: no remote copies, remote signals or barrier semaphores. Data moves between devices by JAX's collectives and lax.ppermute only.
A program may use at most 64 MiB of HBM per device.

```python
import jax
import jax.numpy as jnp
from jax import lax

D = 1024
M = 64
K = 256
DS = 16
ROW_DEV = 2560
BLOCKS = 32
ROWS = 81920


def shared_codes(key):
    return jax.random.randint(jax.random.fold_in(key, 7), (ROWS, M), 0, K, dtype=jnp.int32)


def draw_codes(key, part):
    return shared_codes(key)


def draw_vectors(key, part):
    codes = shared_codes(key)
    table = jax.random.normal(jax.random.fold_in(key, 11), (K, D), jnp.float32)
    spread = jnp.repeat(codes, DS, axis=1)
    offset = table[spread, jnp.arange(D)[None, :]]
    values = jax.random.normal(jax.random.fold_in(key, 13), (ROWS, D), jnp.float32) + 1.5 * offset
    return values.astype(jnp.bfloat16)


def draw_rotation(key, part):
    spread = jax.random.normal(key, (D, D), jnp.float32) * 0.5 / D ** 0.5
    return (jnp.eye(D, dtype=jnp.float32) + spread).astype(jnp.bfloat16)


def draw_live_rows(key, part):
    base = jax.random.randint(key, (BLOCKS,), ROW_DEV // 4, ROW_DEV + 1, dtype=jnp.int32)
    where = jax.random.randint(jax.random.fold_in(key, 3), (), 0, BLOCKS, dtype=jnp.int32)
    return jnp.where(jnp.arange(BLOCKS, dtype=jnp.int32) == where, ROW_DEV, base).astype(jnp.int32)


def setup_inputs(seed: int = 0) -> dict:
    key_list = jax.random.split(jax.random.key(seed), 5)
    return {
        "vectors": draw_vectors(jax.random.fold_in(key_list[4], 71), 0),
        "rotation": draw_rotation(jax.random.fold_in(key_list[4], 71), 0),
        "codes": draw_codes(jax.random.fold_in(key_list[4], 71), 0),
        "live_rows": draw_live_rows(jax.random.fold_in(key_list[4], 71), 0),
    }


def make_hot(code_block, live):
    keep = (jnp.arange(ROW_DEV, dtype=jnp.int32) < live).astype(jnp.float32)
    kinds = jnp.arange(K, dtype=jnp.int32)
    hot = (code_block[:, :, None] == kinds[None, None, :]).astype(jnp.float32) * keep[:, None, None]
    return hot.astype(jnp.bfloat16)


def reference(vectors, rotation, codes, live_rows):
    vector_blocks = vectors.reshape(BLOCKS, ROW_DEV, D)
    code_blocks = codes.reshape(BLOCKS, ROW_DEV, M)

    def first(carry, item):
        block, code_block, live = item
        rotated = jnp.dot(block, rotation, preferred_element_type=jnp.float32)
        hot = make_hot(code_block, live).astype(jnp.float32)
        pieces = rotated.reshape(ROW_DEV, M, DS)
        sums = jnp.einsum("nmk,nmd->kmd", hot, pieces, precision=lax.Precision.HIGHEST).reshape(K, D)
        counts = jnp.sum(hot, axis=0).T
        return (carry[0] + sums, carry[1] + counts), None

    start = (jnp.zeros((K, D), jnp.float32), jnp.zeros((K, M), jnp.float32))
    totals, unused = lax.scan(first, start, (vector_blocks, code_blocks, live_rows))
    sums, counts = totals
    centroids = sums / (jnp.repeat(counts, DS, axis=1) + 1.0)
    table = centroids.astype(jnp.bfloat16).astype(jnp.float32).reshape(K, M, DS)

    def second(carry, item):
        block, code_block, live = item
        hot = make_hot(code_block, live).astype(jnp.float32)
        recon = jnp.einsum("nmk,kmd->nmd", hot, table).reshape(ROW_DEV, D).astype(jnp.bfloat16)
        return carry + jnp.dot(recon.T, block, preferred_element_type=jnp.float32), None

    grad_sum, unused = lax.scan(second, jnp.zeros((D, D), jnp.float32), (vector_blocks, code_blocks, live_rows))
    return centroids, grad_sum / ROWS
```

```python
import jax
import jax.numpy as jnp
import numpy as np
from jax import lax
from jax.sharding import Mesh
from jax.sharding import PartitionSpec as P

K = 256
DS = 16

ROW_PARTS = (("z", 8), ("xl", 2), ("c", 2))
FEAT_PARTS = (("y", 4), ("xh", 2))
REDUCE_ORDER = ("c", "xl", "z")
FLAT_ROW_SUMS = False


def split_hi_lo(x):
    hi = x.astype(jnp.bfloat16)
    lo = (x - hi.astype(jnp.float32)).astype(jnp.bfloat16)
    return hi, lo


def row_psum(x, row_names, order):
    if FLAT_ROW_SUMS:
        return lax.psum(x, row_names)
    for name in order:
        x = lax.psum(x, name)
    return x


def shards(vectors, rotation, codes, live_rows, *, row_names, feat_names, row_sizes, order):
    rows = vectors.shape[0]
    local = vectors.shape[1]
    groups = codes.shape[1]
    n_feat = rotation.shape[1] // local
    n_row = int(np.prod(row_sizes))

    full = lax.all_gather(vectors, feat_names, axis=1, tiled=True)
    columns = lax.all_to_all(rotation, feat_names, split_axis=1, concat_axis=0, tiled=True)
    rotated = jnp.dot(full, columns, preferred_element_type=jnp.float32)

    keep = (jnp.arange(rows, dtype=jnp.int32) < live_rows[0]).astype(jnp.bfloat16)
    kinds = jnp.arange(K, dtype=jnp.int32)
    hot = (codes[:, :, None] == kinds[None, None, :]).astype(jnp.bfloat16) * keep[:, None, None]
    hot = hot.reshape(rows, groups * K)

    hi, lo = split_hi_lo(rotated)
    rhs = jnp.concatenate([hi, lo, keep[:, None]], axis=1)
    both = lax.dot_general(hot, rhs, (((0,), (0,)), ((), ())), preferred_element_type=jnp.float32)
    blocks = (both[:, :local] + both[:, local : 2 * local]).reshape(groups, K, groups, DS)
    picks = jnp.arange(groups)
    sums = blocks[picks, :, picks, :]
    counts = both[:, 2 * local].reshape(groups, K)
    packed = jnp.concatenate([sums.reshape(groups, K * DS), counts], axis=1)

    packed = row_psum(packed, row_names, order)
    total_sums = packed[:, : K * DS].reshape(groups, K, DS)
    total_counts = packed[:, K * DS :]
    cents = total_sums / (total_counts[:, :, None] + 1.0)
    centroids_all = cents.transpose(1, 0, 2).reshape(K, groups * DS)

    row_index = lax.axis_index(row_names)
    share = K // n_row
    centroids = lax.dynamic_slice_in_dim(centroids_all, row_index * share, share, 0)

    table = cents.astype(jnp.bfloat16)
    eye = jnp.eye(groups, dtype=jnp.bfloat16)
    diag = (table[:, :, None, :] * eye[:, None, :, None]).reshape(groups * K, groups * DS)
    recon = jnp.dot(hot, diag, preferred_element_type=jnp.float32).astype(jnp.bfloat16)

    inverse = 1.0 / (rows * n_row)
    product = lax.dot_general(
        recon, full, (((0,), (0,)), ((), ())), preferred_element_type=jnp.float32
    )
    product = product * inverse

    grad_rows = (groups * DS * n_feat) // n_row
    parts = local // grad_rows
    pieces = product.reshape(parts, grad_rows, n_feat, local).transpose(0, 2, 1, 3)
    pieces = pieces.reshape(parts * n_feat, grad_rows, local)
    for name in order:
        pieces = lax.psum_scatter(pieces, name, scatter_dimension=0, tiled=True)
    piece = pieces[0]

    perm = []
    sizes = dict(zip(row_names, row_sizes))
    for r in range(n_row):
        coords = {}
        rest = r
        for name, size in reversed(list(zip(row_names, row_sizes))):
            coords[name] = rest % size
            rest //= size
        p = 0
        for name in order:
            p = p * sizes[name] + coords[name]
        a, f = divmod(p, n_feat)
        for src_feat in range(n_feat):
            dst_row = src_feat * parts + a
            perm.append((r * n_feat + src_feat, dst_row * n_feat + f))
    grad_t = lax.ppermute(piece, row_names + feat_names, perm)
    return centroids, grad_t


def solution(mesh):
    row_size = mesh.shape["row"]
    feat_size = mesh.shape["feat"]
    row_sizes = tuple(s for _, s in ROW_PARTS)
    feat_sizes = tuple(s for _, s in FEAT_PARTS)
    if int(np.prod(row_sizes)) != row_size or int(np.prod(feat_sizes)) != feat_size:
        row_parts, feat_parts = (("row", row_size),), (("feat", feat_size),)
    else:
        row_parts, feat_parts = ROW_PARTS, FEAT_PARTS
    names = tuple(n for n, _ in row_parts + feat_parts)
    shape = tuple(s for _, s in row_parts + feat_parts)
    fine = Mesh(np.asarray(mesh.devices).reshape(shape), names)
    row_names = tuple(n for n, _ in row_parts)
    feat_names = tuple(n for n, _ in feat_parts)

    def body(vectors, rotation, codes, live_rows):
        return shards(
            vectors,
            rotation,
            codes,
            live_rows,
            row_names=row_names,
            feat_names=feat_names,
            row_sizes=tuple(s for _, s in row_parts),
            order=REDUCE_ORDER if row_parts is ROW_PARTS else row_names,
        )

    return jax.shard_map(
        body,
        mesh=fine,
        in_specs=(P(row_names, feat_names), P(feat_names, None), P(row_names, feat_names), P(row_names)),
        out_specs=(P(row_names, feat_names), P(row_names, feat_names)),
        check_vma=False,
    )
```

```python
import jax
import jax.numpy as jnp
import numpy as np
from jax import lax
from jax.sharding import Mesh
from jax.sharding import PartitionSpec as P

K = 256
DS = 16

ROW_PARTS = (("z", 8), ("xl", 2), ("c", 2))
FEAT_PARTS = (("y", 4), ("xh", 2))
REDUCE_ORDER = ("c", "xl", "z")


def axis_bit(name, bit):
    return (lax.axis_index(name) >> bit) & 1


def steps_of(row_names, row_sizes, order):
    sizes = dict(zip(row_names, row_sizes))
    out = []
    for name in order:
        for bit in range(int(sizes[name]).bit_length() - 1):
            out.append((name, bit, sizes[name]))
    return out


def exchange(x, name, bit, size):
    pairs = [(i, i ^ (1 << bit)) for i in range(size)]
    return lax.ppermute(x, name, pairs)


def row_psum(x, steps):
    for name, bit, size in steps:
        x = x + exchange(x, name, bit, size)
    return x


def row_psum_scatter(x, steps):
    for name, bit, size in steps:
        halves = x.reshape((2, x.shape[0] // 2) + x.shape[1:])
        mine = axis_bit(name, bit)
        keep = lax.dynamic_index_in_dim(halves, mine, 0, keepdims=False)
        send = lax.dynamic_index_in_dim(halves, 1 - mine, 0, keepdims=False)
        x = keep + exchange(send, name, bit, size)
    return x


def shards(vectors, rotation, codes, live_rows, *, row_names, feat_names, row_sizes, order):
    rows = vectors.shape[0]
    local = vectors.shape[1]
    groups = codes.shape[1]
    n_feat = rotation.shape[1] // local
    n_row = int(np.prod(row_sizes))
    steps = steps_of(row_names, row_sizes, order)

    full = lax.all_gather(vectors, feat_names, axis=1, tiled=True)
    columns = lax.all_to_all(rotation, feat_names, split_axis=1, concat_axis=0, tiled=True)
    rotated = jnp.dot(full, columns, preferred_element_type=jnp.float32)

    keep = (jnp.arange(rows, dtype=jnp.int32) < live_rows[0]).astype(jnp.bfloat16)
    kinds = jnp.arange(K, dtype=jnp.int32)
    hot = (codes.T[:, None, :] == kinds[None, :, None]).astype(jnp.bfloat16) * keep[None, None, :]
    hot = hot.reshape(groups * K, rows)

    hi = lax.reduce_precision(rotated, exponent_bits=8, mantissa_bits=7)
    lo = (rotated - hi).astype(jnp.bfloat16)
    rhs = jnp.concatenate([hi.astype(jnp.bfloat16), lo, keep[:, None]], axis=1)
    both = jnp.dot(hot, rhs, preferred_element_type=jnp.float32)
    blocks = (both[:, :local] + both[:, local : 2 * local]).reshape(groups, K, groups, DS)
    picks = jnp.arange(groups)
    sums = blocks[picks, :, picks, :]
    counts = both[:, 2 * local].reshape(groups, K)
    packed = jnp.concatenate([sums.reshape(groups, K * DS), counts], axis=1)

    packed = row_psum(packed, steps)
    total_sums = packed[:, : K * DS].reshape(groups, K, DS)
    total_counts = packed[:, K * DS :]
    cents = total_sums / (total_counts[:, :, None] + 1.0)
    centroids_all = cents.transpose(1, 0, 2).reshape(K, groups * DS)

    row_index = lax.axis_index(row_names)
    share = K // n_row
    centroids = lax.dynamic_slice_in_dim(centroids_all, row_index * share, share, 0)

    table = cents.astype(jnp.bfloat16)
    eye = jnp.eye(groups, dtype=jnp.bfloat16)
    diag_t = (table.transpose(0, 2, 1)[:, :, None, :] * eye[:, None, :, None]).reshape(
        groups * DS, groups * K
    )
    recon_t = jnp.dot(diag_t, hot, preferred_element_type=jnp.float32).astype(jnp.bfloat16)

    inverse = 1.0 / (rows * n_row)
    product = jnp.dot(recon_t, full, preferred_element_type=jnp.float32)
    product = product * inverse

    grad_rows = (groups * DS * n_feat) // n_row
    parts = local // grad_rows
    pieces = product.reshape(parts, grad_rows, n_feat, local).transpose(0, 2, 1, 3)
    pieces = pieces.reshape(parts * n_feat, grad_rows, local)
    piece = row_psum_scatter(pieces, steps)[0]

    perm = []
    for r in range(n_row):
        coords = {}
        rest = r
        for name, size in reversed(list(zip(row_names, row_sizes))):
            coords[name] = rest % size
            rest //= size
        q = 0
        for name, bit, size in steps:
            q = q * 2 + ((coords[name] >> bit) & 1)
        a, f = divmod(q, n_feat)
        for src_feat in range(n_feat):
            dst_row = src_feat * parts + a
            perm.append((r * n_feat + src_feat, dst_row * n_feat + f))
    grad_t = lax.ppermute(piece, row_names + feat_names, perm)
    return centroids, grad_t


def solution(mesh):
    row_size = mesh.shape["row"]
    feat_size = mesh.shape["feat"]
    row_sizes = tuple(s for _, s in ROW_PARTS)
    feat_sizes = tuple(s for _, s in FEAT_PARTS)
    if int(np.prod(row_sizes)) != row_size or int(np.prod(feat_sizes)) != feat_size:
        row_parts, feat_parts = (("row", row_size),), (("feat", feat_size),)
    else:
        row_parts, feat_parts = ROW_PARTS, FEAT_PARTS
    names = tuple(n for n, _ in row_parts + feat_parts)
    shape = tuple(s for _, s in row_parts + feat_parts)
    fine = Mesh(np.asarray(mesh.devices).reshape(shape), names)
    row_names = tuple(n for n, _ in row_parts)
    feat_names = tuple(n for n, _ in feat_parts)

    def body(vectors, rotation, codes, live_rows):
        return shards(
            vectors,
            rotation,
            codes,
            live_rows,
            row_names=row_names,
            feat_names=feat_names,
            row_sizes=tuple(s for _, s in row_parts),
            order=REDUCE_ORDER if row_parts is ROW_PARTS else row_names,
        )

    return jax.shard_map(
        body,
        mesh=fine,
        in_specs=(P(row_names, feat_names), P(feat_names, None), P(row_names, feat_names), P(row_names)),
        out_specs=(P(row_names, feat_names), P(row_names, feat_names)),
        check_vma=False,
    )
```

```python
import jax
import jax.numpy as jnp
import numpy as np
from jax import lax
from jax.sharding import Mesh
from jax.sharding import PartitionSpec as P

K = 256
DS = 16

ROW_PARTS = (("z", 8), ("xl", 2), ("c", 2))
FEAT_PARTS = (("y", 4), ("xh", 2))
REDUCE_ORDER = ("c", "xl", "z")
GATHER_BY_ALL_TO_ALL = True


def axis_bit(name, bit):
    return (lax.axis_index(name) >> bit) & 1


def steps_of(row_names, row_sizes, order):
    sizes = dict(zip(row_names, row_sizes))
    out = []
    for name in order:
        for bit in range(int(sizes[name]).bit_length() - 1):
            out.append((name, bit, sizes[name]))
    return out


def exchange(x, name, bit, size):
    pairs = [(i, i ^ (1 << bit)) for i in range(size)]
    return lax.ppermute(x, name, pairs)


def row_psum(x, steps):
    for name, bit, size in steps:
        x = x + exchange(x, name, bit, size)
    return x


def row_psum_scatter(x, steps):
    for name, bit, size in steps:
        halves = x.reshape((2, x.shape[0] // 2) + x.shape[1:])
        mine = axis_bit(name, bit)
        keep = lax.dynamic_index_in_dim(halves, mine, 0, keepdims=False)
        send = lax.dynamic_index_in_dim(halves, 1 - mine, 0, keepdims=False)
        x = keep + exchange(send, name, bit, size)
    return x


def shards(vectors, rotation, codes, live_rows, *, row_names, feat_names, row_sizes, order):
    rows = vectors.shape[0]
    local = vectors.shape[1]
    groups = codes.shape[1]
    n_feat = rotation.shape[1] // local
    n_row = int(np.prod(row_sizes))
    steps = steps_of(row_names, row_sizes, order)

    if GATHER_BY_ALL_TO_ALL:
        copies = jnp.broadcast_to(vectors[None], (n_feat,) + vectors.shape)
        blocks_in = lax.all_to_all(copies, feat_names, split_axis=0, concat_axis=0, tiled=True)
    else:
        full = lax.all_gather(vectors, feat_names, axis=1, tiled=True)
        blocks_in = full.reshape(rows, n_feat, local).transpose(1, 0, 2)
    columns = lax.all_to_all(rotation, feat_names, split_axis=1, concat_axis=0, tiled=True)
    columns = columns.reshape(n_feat, local, local)
    rotated = lax.dot_general(
        blocks_in, columns, (((0, 2), (0, 1)), ((), ())), preferred_element_type=jnp.float32
    )

    keep = (jnp.arange(rows, dtype=jnp.int32) < live_rows[0]).astype(jnp.bfloat16)
    kinds = jnp.arange(K, dtype=jnp.int32)
    hot = (codes.T[:, None, :] == kinds[None, :, None]).astype(jnp.bfloat16) * keep[None, None, :]
    hot = hot.reshape(groups * K, rows)

    hi = lax.reduce_precision(rotated, exponent_bits=8, mantissa_bits=7)
    lo = (rotated - hi).astype(jnp.bfloat16)
    rhs = jnp.concatenate([hi.astype(jnp.bfloat16), lo, keep[:, None]], axis=1)
    both = jnp.dot(hot, rhs, preferred_element_type=jnp.float32)
    blocks = (both[:, :local] + both[:, local : 2 * local]).reshape(groups, K, groups, DS)
    picks = jnp.arange(groups)
    sums = blocks[picks, :, picks, :]
    counts = both[:, 2 * local].reshape(groups, K)
    packed = jnp.concatenate([sums.reshape(groups, K * DS), counts], axis=1)

    packed = row_psum(packed, steps)
    total_sums = packed[:, : K * DS].reshape(groups, K, DS)
    total_counts = packed[:, K * DS :]
    cents = total_sums / (total_counts[:, :, None] + 1.0)
    centroids_all = cents.transpose(1, 0, 2).reshape(K, groups * DS)

    row_index = lax.axis_index(row_names)
    share = K // n_row
    centroids = lax.dynamic_slice_in_dim(centroids_all, row_index * share, share, 0)

    table = cents.astype(jnp.bfloat16)
    eye = jnp.eye(groups, dtype=jnp.bfloat16)
    diag_t = (table.transpose(0, 2, 1)[:, :, None, :] * eye[:, None, :, None]).reshape(
        groups * DS, groups * K
    )
    recon_t = jnp.dot(diag_t, hot, preferred_element_type=jnp.float32).astype(jnp.bfloat16)

    inverse = 1.0 / (rows * n_row)
    product = lax.dot_general(
        recon_t, blocks_in, (((1,), (1,)), ((), ())), preferred_element_type=jnp.float32
    )
    product = product * inverse

    grad_rows = (groups * DS * n_feat) // n_row
    parts = local // grad_rows
    pieces = product.reshape(parts, grad_rows, n_feat, local).transpose(0, 2, 1, 3)
    pieces = pieces.reshape(parts * n_feat, grad_rows, local)
    piece = row_psum_scatter(pieces, steps)[0]

    perm = []
    for r in range(n_row):
        coords = {}
        rest = r
        for name, size in reversed(list(zip(row_names, row_sizes))):
            coords[name] = rest % size
            rest //= size
        q = 0
        for name, bit, size in steps:
            q = q * 2 + ((coords[name] >> bit) & 1)
        a, f = divmod(q, n_feat)
        for src_feat in range(n_feat):
            dst_row = src_feat * parts + a
            perm.append((r * n_feat + src_feat, dst_row * n_feat + f))
    grad_t = lax.ppermute(piece, row_names + feat_names, perm)
    return centroids, grad_t


def solution(mesh):
    row_size = mesh.shape["row"]
    feat_size = mesh.shape["feat"]
    row_sizes = tuple(s for _, s in ROW_PARTS)
    feat_sizes = tuple(s for _, s in FEAT_PARTS)
    if int(np.prod(row_sizes)) != row_size or int(np.prod(feat_sizes)) != feat_size:
        row_parts, feat_parts = (("row", row_size),), (("feat", feat_size),)
    else:
        row_parts, feat_parts = ROW_PARTS, FEAT_PARTS
    names = tuple(n for n, _ in row_parts + feat_parts)
    shape = tuple(s for _, s in row_parts + feat_parts)
    fine = Mesh(np.asarray(mesh.devices).reshape(shape), names)
    row_names = tuple(n for n, _ in row_parts)
    feat_names = tuple(n for n, _ in feat_parts)

    def body(vectors, rotation, codes, live_rows):
        return shards(
            vectors,
            rotation,
            codes,
            live_rows,
            row_names=row_names,
            feat_names=feat_names,
            row_sizes=tuple(s for _, s in row_parts),
            order=REDUCE_ORDER if row_parts is ROW_PARTS else row_names,
        )

    return jax.shard_map(
        body,
        mesh=fine,
        in_specs=(P(row_names, feat_names), P(feat_names, None), P(row_names, feat_names), P(row_names)),
        out_specs=(P(row_names, feat_names), P(row_names, feat_names)),
        check_vma=False,
    )
```

```python
import jax
import jax.numpy as jnp
import numpy as np
from jax import lax
from jax.sharding import Mesh
from jax.sharding import PartitionSpec as P

K = 256
DS = 16

ROW_PARTS = (("z", 8), ("xl", 2), ("c", 2))
FEAT_PARTS = (("y", 4), ("xh", 2))
REDUCE_ORDER = ("c", "xl", "z")


def axis_bit(name, bit):
    return (lax.axis_index(name) >> bit) & 1


def steps_of(row_names, row_sizes, order):
    sizes = dict(zip(row_names, row_sizes))
    out = []
    for name in order:
        for bit in range(int(sizes[name]).bit_length() - 1):
            out.append((name, bit, sizes[name]))
    return out


def exchange(x, name, bit, size):
    pairs = [(i, i ^ (1 << bit)) for i in range(size)]
    return lax.ppermute(x, name, pairs)


def row_psum(x, steps):
    for name, bit, size in steps:
        x = x + exchange(x, name, bit, size)
    return x


def row_psum_scatter(x, steps):
    for name, bit, size in steps:
        halves = x.reshape((2, x.shape[0] // 2) + x.shape[1:])
        mine = axis_bit(name, bit)
        keep = lax.dynamic_index_in_dim(halves, mine, 0, keepdims=False)
        send = lax.dynamic_index_in_dim(halves, 1 - mine, 0, keepdims=False)
        x = keep + exchange(send, name, bit, size)
    return x


def shards(vectors, rotation, codes, live_rows, *, row_names, feat_names, row_sizes, order):
    rows = vectors.shape[0]
    local = vectors.shape[1]
    groups = codes.shape[1]
    n_feat = rotation.shape[1] // local
    n_row = int(np.prod(row_sizes))
    steps = steps_of(row_names, row_sizes, order)

    copies = jnp.broadcast_to(vectors[None], (n_feat,) + vectors.shape)
    rotation_blocks = rotation.reshape(local, n_feat, local).transpose(1, 0, 2)
    outgoing = jnp.concatenate([copies, rotation_blocks], axis=1)
    incoming = lax.all_to_all(outgoing, feat_names, split_axis=0, concat_axis=0, tiled=True)
    blocks_in = incoming[:, :rows]
    columns = incoming[:, rows:]
    rotated = lax.dot_general(
        blocks_in, columns, (((0, 2), (0, 1)), ((), ())), preferred_element_type=jnp.float32
    )

    keep = (jnp.arange(rows, dtype=jnp.int32) < live_rows[0]).astype(jnp.bfloat16)
    kinds = jnp.arange(K, dtype=jnp.int32)
    hot = (codes.T[:, None, :] == kinds[None, :, None]).astype(jnp.bfloat16) * keep[None, None, :]
    hot = hot.reshape(groups * K, rows)

    hi = lax.reduce_precision(rotated, exponent_bits=8, mantissa_bits=7)
    lo = (rotated - hi).astype(jnp.bfloat16)
    rhs = jnp.concatenate([hi.astype(jnp.bfloat16), lo, keep[:, None]], axis=1)
    both = jnp.dot(hot, rhs, preferred_element_type=jnp.float32)
    blocks = (both[:, :local] + both[:, local : 2 * local]).reshape(groups, K, groups, DS)
    picks = jnp.arange(groups)
    sums = blocks[picks, :, picks, :]
    counts = both[:, 2 * local].reshape(groups, K)
    packed = jnp.concatenate([sums.reshape(groups, K * DS), counts], axis=1)

    packed = row_psum(packed, steps)
    total_sums = packed[:, : K * DS].reshape(groups, K, DS)
    total_counts = packed[:, K * DS :]
    cents = total_sums / (total_counts[:, :, None] + 1.0)
    centroids_all = cents.transpose(1, 0, 2).reshape(K, groups * DS)

    row_index = lax.axis_index(row_names)
    share = K // n_row
    centroids = lax.dynamic_slice_in_dim(centroids_all, row_index * share, share, 0)

    table = cents.astype(jnp.bfloat16)
    eye = jnp.eye(groups, dtype=jnp.bfloat16)
    diag_t = (table.transpose(0, 2, 1)[:, :, None, :] * eye[:, None, :, None]).reshape(
        groups * DS, groups * K
    )
    recon_t = jnp.dot(diag_t, hot, preferred_element_type=jnp.float32).astype(jnp.bfloat16)

    inverse = 1.0 / (rows * n_row)
    product = lax.dot_general(
        recon_t, blocks_in, (((1,), (1,)), ((), ())), preferred_element_type=jnp.float32
    )
    product = product * inverse

    grad_rows = (groups * DS * n_feat) // n_row
    parts = local // grad_rows
    pieces = product.reshape(parts, grad_rows, n_feat, local).transpose(0, 2, 1, 3)
    pieces = pieces.reshape(parts * n_feat, grad_rows, local)
    piece = row_psum_scatter(pieces, steps)[0]

    perm = []
    for r in range(n_row):
        coords = {}
        rest = r
        for name, size in reversed(list(zip(row_names, row_sizes))):
            coords[name] = rest % size
            rest //= size
        q = 0
        for name, bit, size in steps:
            q = q * 2 + ((coords[name] >> bit) & 1)
        a, f = divmod(q, n_feat)
        for src_feat in range(n_feat):
            dst_row = src_feat * parts + a
            perm.append((r * n_feat + src_feat, dst_row * n_feat + f))
    grad_t = lax.ppermute(piece, row_names + feat_names, perm)
    return centroids, grad_t


def solution(mesh):
    row_size = mesh.shape["row"]
    feat_size = mesh.shape["feat"]
    row_sizes = tuple(s for _, s in ROW_PARTS)
    feat_sizes = tuple(s for _, s in FEAT_PARTS)
    if int(np.prod(row_sizes)) != row_size or int(np.prod(feat_sizes)) != feat_size:
        row_parts, feat_parts = (("row", row_size),), (("feat", feat_size),)
    else:
        row_parts, feat_parts = ROW_PARTS, FEAT_PARTS
    names = tuple(n for n, _ in row_parts + feat_parts)
    shape = tuple(s for _, s in row_parts + feat_parts)
    fine = Mesh(np.asarray(mesh.devices).reshape(shape), names)
    row_names = tuple(n for n, _ in row_parts)
    feat_names = tuple(n for n, _ in feat_parts)

    def body(vectors, rotation, codes, live_rows):
        return shards(
            vectors,
            rotation,
            codes,
            live_rows,
            row_names=row_names,
            feat_names=feat_names,
            row_sizes=tuple(s for _, s in row_parts),
            order=REDUCE_ORDER if row_parts is ROW_PARTS else row_names,
        )

    return jax.shard_map(
        body,
        mesh=fine,
        in_specs=(P(row_names, feat_names), P(feat_names, None), P(row_names, feat_names), P(row_names)),
        out_specs=(P(row_names, feat_names), P(row_names, feat_names)),
        check_vma=False,
    )
```

```python
import functools

import jax
import jax.numpy as jnp
import numpy as np
from jax import lax
from jax.experimental import pallas as pl
from jax.sharding import Mesh
from jax.sharding import PartitionSpec as P

K = 256
DS = 16

ROW_PARTS = (("z", 8), ("xl", 2), ("c", 2))
FEAT_PARTS = (("y", 4), ("xh", 2))
REDUCE_ORDER = ("c", "xl", "z")
GROUP = 8


def axis_bit(name, bit):
    return (lax.axis_index(name) >> bit) & 1


def steps_of(row_names, row_sizes, order):
    sizes = dict(zip(row_names, row_sizes))
    out = []
    for name in order:
        for bit in range(int(sizes[name]).bit_length() - 1):
            out.append((name, bit, sizes[name]))
    return out


def exchange(x, name, bit, size):
    pairs = [(i, i ^ (1 << bit)) for i in range(size)]
    return lax.ppermute(x, name, pairs)


def row_psum(x, steps):
    for name, bit, size in steps:
        x = x + exchange(x, name, bit, size)
    return x


def row_psum_scatter(x, steps):
    for name, bit, size in steps:
        halves = x.reshape((2, x.shape[0] // 2) + x.shape[1:])
        mine = axis_bit(name, bit)
        keep = lax.dynamic_index_in_dim(halves, mine, 0, keepdims=False)
        send = lax.dynamic_index_in_dim(halves, 1 - mine, 0, keepdims=False)
        x = keep + exchange(send, name, bit, size)
    return x


def means_kernel(codes_ref, vec_ref, hi_ref, lo_ref):
    rows = codes_ref.shape[1]
    kinds = lax.broadcasted_iota(jnp.int32, (K, rows), 0)
    one = jnp.ones((K, rows), jnp.bfloat16)
    zero = jnp.zeros((K, rows), jnp.bfloat16)
    for i in range(codes_ref.shape[0]):
        hot = jnp.where(codes_ref[pl.ds(i, 1), :] == kinds, one, zero)
        h = jnp.dot(hot, vec_ref[...], preferred_element_type=jnp.float32)
        hi = h.astype(jnp.bfloat16)
        hi_ref[i] = hi
        lo_ref[i] = (h - hi.astype(jnp.float32)).astype(jnp.bfloat16)


def codeword_means(codes_all, vectors):
    m_all, rows = codes_all.shape
    width = vectors.shape[1]
    out = jax.ShapeDtypeStruct((m_all, K, width), jnp.bfloat16)
    return pl.pallas_call(
        means_kernel,
        grid=(m_all // GROUP,),
        in_specs=[
            pl.BlockSpec((GROUP, rows), lambda g: (g, 0)),
            pl.BlockSpec((rows, width), lambda g: (0, 0)),
        ],
        out_specs=[
            pl.BlockSpec((GROUP, K, width), lambda g: (g, 0, 0)),
            pl.BlockSpec((GROUP, K, width), lambda g: (g, 0, 0)),
        ],
        out_shape=[out, out],
        cost_estimate=pl.CostEstimate(
            flops=2 * m_all * K * rows * width,
            transcendentals=0,
            bytes_accessed=codes_all.size * 4 + vectors.size * 2 + 2 * m_all * K * width * 2,
        ),
    )(codes_all, vectors)


def broadcast_over(x, names, count):
    copies = jnp.broadcast_to(x[None], (count,) + x.shape)
    return lax.all_to_all(copies, names, split_axis=0, concat_axis=0, tiled=True)


def shards(vectors, rotation, codes, live_rows, *, row_names, feat_names, row_sizes, order):
    rows = vectors.shape[0]
    local = vectors.shape[1]
    groups = codes.shape[1]
    n_feat = rotation.shape[1] // local
    m_all = groups * n_feat
    n_row = int(np.prod(row_sizes))
    steps = steps_of(row_names, row_sizes, order)

    keep = jnp.arange(rows, dtype=jnp.int32) < live_rows[0]
    masked = jnp.where(keep[:, None], codes, -1).T
    codes_all = broadcast_over(masked, feat_names, n_feat).reshape(m_all, rows)

    kinds = jnp.arange(K, dtype=jnp.int32)
    counts = jnp.sum(
        (masked[:, None, :] == kinds[None, :, None]).astype(jnp.float32), axis=2
    )

    h_hi, h_lo = codeword_means(codes_all, vectors)

    rot3 = rotation.reshape(local, m_all, DS).transpose(1, 0, 2)
    dims = (((2,), (1,)), ((0,), (0,)))
    partial = lax.dot_general(h_hi, rot3, dims, preferred_element_type=jnp.float32)
    partial = partial + lax.dot_general(h_lo, rot3, dims, preferred_element_type=jnp.float32)

    partial = partial.reshape(n_feat, groups, K, DS)
    sums = jnp.sum(
        lax.all_to_all(partial, feat_names, split_axis=0, concat_axis=0, tiled=True), axis=0
    )
    packed = jnp.concatenate([sums.reshape(groups, K * DS), counts], axis=1)

    packed = row_psum(packed, steps)
    total_sums = packed[:, : K * DS].reshape(groups, K, DS)
    total_counts = packed[:, K * DS :]
    cents = total_sums / (total_counts[:, :, None] + 1.0)
    centroids_all = cents.transpose(1, 0, 2).reshape(K, groups * DS)

    row_index = lax.axis_index(row_names)
    share = K // n_row
    centroids = lax.dynamic_slice_in_dim(centroids_all, row_index * share, share, 0)

    table = broadcast_over(cents.astype(jnp.bfloat16), feat_names, n_feat)
    table = table.reshape(m_all, K, DS)
    dims = (((1,), (1,)), ((0,), (0,)))
    grad = lax.dot_general(table, h_hi, dims, preferred_element_type=jnp.float32)
    grad = grad + lax.dot_general(table, h_lo, dims, preferred_element_type=jnp.float32)
    inverse = 1.0 / (rows * n_row)
    grad = grad.reshape(m_all * DS, local) * inverse

    grad_rows = (m_all * DS) // n_row
    pieces = grad.reshape(n_row, grad_rows, local)
    position = []
    for r in range(n_row):
        coords = {}
        rest = r
        for name, size in reversed(list(zip(row_names, row_sizes))):
            coords[name] = rest % size
            rest //= size
        q = 0
        for name, bit, size in steps:
            q = q * 2 + ((coords[name] >> bit) & 1)
        position.append((q, r))
    source = np.array([r for _, r in sorted(position)], dtype=np.int32)
    pieces = pieces[source]
    grad_t = row_psum_scatter(pieces, steps)[0]
    return centroids, grad_t


def solution(mesh):
    row_size = mesh.shape["row"]
    feat_size = mesh.shape["feat"]
    row_sizes = tuple(s for _, s in ROW_PARTS)
    feat_sizes = tuple(s for _, s in FEAT_PARTS)
    if int(np.prod(row_sizes)) != row_size or int(np.prod(feat_sizes)) != feat_size:
        row_parts, feat_parts = (("row", row_size),), (("feat", feat_size),)
    else:
        row_parts, feat_parts = ROW_PARTS, FEAT_PARTS
    names = tuple(n for n, _ in row_parts + feat_parts)
    shape = tuple(s for _, s in row_parts + feat_parts)
    fine = Mesh(np.asarray(mesh.devices).reshape(shape), names)
    row_names = tuple(n for n, _ in row_parts)
    feat_names = tuple(n for n, _ in feat_parts)

    body = functools.partial(
        shards,
        row_names=row_names,
        feat_names=feat_names,
        row_sizes=tuple(s for _, s in row_parts),
        order=REDUCE_ORDER if row_parts is ROW_PARTS else row_names,
    )
    return jax.shard_map(
        body,
        mesh=fine,
        in_specs=(P(row_names, feat_names), P(feat_names, None), P(row_names, feat_names), P(row_names)),
        out_specs=(P(row_names, feat_names), P(row_names, feat_names)),
        check_vma=False,
    )
```

```python
import functools

import jax
import jax.numpy as jnp
import numpy as np
from jax import lax
from jax.experimental import pallas as pl
from jax.sharding import Mesh
from jax.sharding import PartitionSpec as P

K = 256
DS = 16

ROW_PARTS = (("z", 8), ("xl", 2), ("c", 2))
FEAT_PARTS = (("y", 4), ("xh", 2))
REDUCE_ORDER = ("c", "xl", "z")
GROUP = 8


def axis_bit(name, bit):
    return (lax.axis_index(name) >> bit) & 1


def steps_of(row_names, row_sizes, order):
    sizes = dict(zip(row_names, row_sizes))
    out = []
    for name in order:
        for bit in range(int(sizes[name]).bit_length() - 1):
            out.append((name, bit, sizes[name]))
    return out


def exchange(x, name, bit, size):
    pairs = [(i, i ^ (1 << bit)) for i in range(size)]
    return lax.ppermute(x, name, pairs)


def row_psum(x, steps):
    for name, bit, size in steps:
        x = x + exchange(x, name, bit, size)
    return x


def row_psum_scatter(x, steps):
    for name, bit, size in steps:
        halves = x.reshape((2, x.shape[0] // 2) + x.shape[1:])
        mine = axis_bit(name, bit)
        keep = lax.dynamic_index_in_dim(halves, mine, 0, keepdims=False)
        send = lax.dynamic_index_in_dim(halves, 1 - mine, 0, keepdims=False)
        x = keep + exchange(send, name, bit, size)
    return x


def means_kernel(codes_ref, vec_ref, hi_ref, lo_ref):
    rows = codes_ref.shape[1]
    kinds = lax.broadcasted_iota(jnp.int32, (K, rows), 0).astype(codes_ref.dtype)
    one = jnp.ones((K, rows), jnp.bfloat16)
    zero = jnp.zeros((K, rows), jnp.bfloat16)
    for i in range(codes_ref.shape[0]):
        hot = jnp.where(codes_ref[pl.ds(i, 1), :] == kinds, one, zero)
        h = jnp.dot(hot, vec_ref[...], preferred_element_type=jnp.float32)
        hi = h.astype(jnp.bfloat16)
        hi_ref[i] = hi
        lo_ref[i] = (h - hi.astype(jnp.float32)).astype(jnp.bfloat16)


def codeword_means(codes_all, vectors):
    m_all, rows = codes_all.shape
    width = vectors.shape[1]
    out = jax.ShapeDtypeStruct((m_all, K, width), jnp.bfloat16)
    return pl.pallas_call(
        means_kernel,
        grid=(m_all // GROUP,),
        in_specs=[
            pl.BlockSpec((GROUP, rows), lambda g: (g, 0)),
            pl.BlockSpec((rows, width), lambda g: (0, 0)),
        ],
        out_specs=[
            pl.BlockSpec((GROUP, K, width), lambda g: (g, 0, 0)),
            pl.BlockSpec((GROUP, K, width), lambda g: (g, 0, 0)),
        ],
        out_shape=[out, out],
        cost_estimate=pl.CostEstimate(
            flops=2 * m_all * K * rows * width,
            transcendentals=0,
            bytes_accessed=codes_all.size * 2 + vectors.size * 2 + 2 * m_all * K * width * 2,
        ),
    )(codes_all, vectors)


def broadcast_over(x, names, count):
    copies = jnp.broadcast_to(x[None], (count,) + x.shape)
    return lax.all_to_all(copies, names, split_axis=0, concat_axis=0, tiled=True)


def shards(vectors, rotation, codes, live_rows, *, row_names, feat_names, row_sizes, order):
    rows = vectors.shape[0]
    local = vectors.shape[1]
    groups = codes.shape[1]
    n_feat = rotation.shape[1] // local
    m_all = groups * n_feat
    n_row = int(np.prod(row_sizes))
    steps = steps_of(row_names, row_sizes, order)

    keep = jnp.arange(rows, dtype=jnp.int32) < live_rows[0]
    masked = jnp.where(keep[:, None], codes, -1).T
    codes_all = broadcast_over(masked.astype(jnp.bfloat16), feat_names, n_feat)
    codes_all = codes_all.reshape(m_all, rows)

    kinds = jnp.arange(K, dtype=jnp.int32)
    counts = jnp.sum(
        (masked[:, None, :] == kinds[None, :, None]).astype(jnp.float32), axis=2
    )

    h_hi, h_lo = codeword_means(codes_all, vectors)

    rot3 = rotation.reshape(local, m_all, DS).transpose(1, 0, 2)
    dims = (((2,), (1,)), ((0,), (0,)))
    partial = lax.dot_general(h_hi, rot3, dims, preferred_element_type=jnp.float32)
    partial = partial + lax.dot_general(h_lo, rot3, dims, preferred_element_type=jnp.float32)

    partial = partial.reshape(n_feat, groups, K, DS)
    sums = jnp.sum(
        lax.all_to_all(partial, feat_names, split_axis=0, concat_axis=0, tiled=True), axis=0
    )
    packed = jnp.concatenate([sums.reshape(groups, K * DS), counts], axis=1)

    packed = row_psum(packed, steps)
    total_sums = packed[:, : K * DS].reshape(groups, K, DS)
    total_counts = packed[:, K * DS :]
    cents = total_sums / (total_counts[:, :, None] + 1.0)
    centroids_all = cents.transpose(1, 0, 2).reshape(K, groups * DS)

    row_index = lax.axis_index(row_names)
    share = K // n_row
    centroids = lax.dynamic_slice_in_dim(centroids_all, row_index * share, share, 0)

    table = broadcast_over(cents.astype(jnp.bfloat16), feat_names, n_feat)
    table = table.reshape(m_all, K, DS)
    dims = (((1,), (1,)), ((0,), (0,)))
    grad = lax.dot_general(table, h_hi, dims, preferred_element_type=jnp.float32)
    grad = grad + lax.dot_general(table, h_lo, dims, preferred_element_type=jnp.float32)
    inverse = 1.0 / (rows * n_row)
    grad = grad.reshape(m_all * DS, local) * inverse

    grad_rows = (m_all * DS) // n_row
    pieces = grad.reshape(n_row, grad_rows, local)
    position = []
    for r in range(n_row):
        coords = {}
        rest = r
        for name, size in reversed(list(zip(row_names, row_sizes))):
            coords[name] = rest % size
            rest //= size
        q = 0
        for name, bit, size in steps:
            q = q * 2 + ((coords[name] >> bit) & 1)
        position.append((q, r))
    source = np.array([r for _, r in sorted(position)], dtype=np.int32)
    pieces = pieces[source]
    grad_t = row_psum_scatter(pieces, steps)[0]
    return centroids, grad_t


def solution(mesh):
    row_size = mesh.shape["row"]
    feat_size = mesh.shape["feat"]
    row_sizes = tuple(s for _, s in ROW_PARTS)
    feat_sizes = tuple(s for _, s in FEAT_PARTS)
    if int(np.prod(row_sizes)) != row_size or int(np.prod(feat_sizes)) != feat_size:
        row_parts, feat_parts = (("row", row_size),), (("feat", feat_size),)
    else:
        row_parts, feat_parts = ROW_PARTS, FEAT_PARTS
    names = tuple(n for n, _ in row_parts + feat_parts)
    shape = tuple(s for _, s in row_parts + feat_parts)
    fine = Mesh(np.asarray(mesh.devices).reshape(shape), names)
    row_names = tuple(n for n, _ in row_parts)
    feat_names = tuple(n for n, _ in feat_parts)

    body = functools.partial(
        shards,
        row_names=row_names,
        feat_names=feat_names,
        row_sizes=tuple(s for _, s in row_parts),
        order=REDUCE_ORDER if row_parts is ROW_PARTS else row_names,
    )
    return jax.shard_map(
        body,
        mesh=fine,
        in_specs=(P(row_names, feat_names), P(feat_names, None), P(row_names, feat_names), P(row_names)),
        out_specs=(P(row_names, feat_names), P(row_names, feat_names)),
        check_vma=False,
    )
```

```python
import functools

import jax
import jax.numpy as jnp
import numpy as np
from jax import lax
from jax.experimental import pallas as pl
from jax.sharding import Mesh
from jax.sharding import PartitionSpec as P

K = 256
DS = 16

ROW_PARTS = (("z", 8), ("xl", 2), ("c", 2))
FEAT_PARTS = (("y", 4), ("xh", 2))
REDUCE_ORDER = ("c", "xl", "z")
RING = ("z", 8)
GROUP = 8


def axis_bit(name, bit):
    return (lax.axis_index(name) >> bit) & 1


def steps_of(row_names, row_sizes, order):
    sizes = dict(zip(row_names, row_sizes))
    out = []
    for name in order:
        for bit in range(int(sizes[name]).bit_length() - 1):
            out.append((name, bit, sizes[name]))
    return out


def exchange(x, name, bit, size):
    pairs = [(i, i ^ (1 << bit)) for i in range(size)]
    return lax.ppermute(x, name, pairs)


def row_psum(x, steps):
    for name, bit, size in steps:
        x = x + exchange(x, name, bit, size)
    return x


def row_psum_scatter(x, steps):
    for name, bit, size in steps:
        halves = x.reshape((2, x.shape[0] // 2) + x.shape[1:])
        mine = axis_bit(name, bit)
        keep = lax.dynamic_index_in_dim(halves, mine, 0, keepdims=False)
        send = lax.dynamic_index_in_dim(halves, 1 - mine, 0, keepdims=False)
        x = keep + exchange(send, name, bit, size)
    return x


def ring_scatter(x, name, size):
    me = lax.axis_index(name)
    total = lax.dynamic_index_in_dim(x, me, 0, keepdims=False)
    for shift in range(1, size):
        part = lax.dynamic_index_in_dim(x, (me + shift) % size, 0, keepdims=False)
        total = total + lax.ppermute(part, name, [(i, (i + shift) % size) for i in range(size)])
    return total


def ring_gather(y, name, size):
    me = lax.axis_index(name)
    out = jnp.zeros((size,) + y.shape, y.dtype)
    out = lax.dynamic_update_index_in_dim(out, y, me, 0)
    for shift in range(1, size):
        got = lax.ppermute(y, name, [(i, (i + shift) % size) for i in range(size)])
        out = lax.dynamic_update_index_in_dim(out, got, (me - shift) % size, 0)
    return out


def means_kernel(codes_ref, vec_ref, hi_ref, lo_ref):
    rows = codes_ref.shape[1]
    kinds = lax.broadcasted_iota(jnp.int32, (K, rows), 0).astype(codes_ref.dtype)
    one = jnp.ones((K, rows), jnp.bfloat16)
    zero = jnp.zeros((K, rows), jnp.bfloat16)
    for i in range(codes_ref.shape[0]):
        hot = jnp.where(codes_ref[pl.ds(i, 1), :] == kinds, one, zero)
        h = jnp.dot(hot, vec_ref[...], preferred_element_type=jnp.float32)
        hi = h.astype(jnp.bfloat16)
        hi_ref[i] = hi
        lo_ref[i] = (h - hi.astype(jnp.float32)).astype(jnp.bfloat16)


def codeword_means(codes_all, vectors):
    m_all, rows = codes_all.shape
    width = vectors.shape[1]
    out = jax.ShapeDtypeStruct((m_all, K, width), jnp.bfloat16)
    return pl.pallas_call(
        means_kernel,
        grid=(m_all // GROUP,),
        in_specs=[
            pl.BlockSpec((GROUP, rows), lambda g: (g, 0)),
            pl.BlockSpec((rows, width), lambda g: (0, 0)),
        ],
        out_specs=[
            pl.BlockSpec((GROUP, K, width), lambda g: (g, 0, 0)),
            pl.BlockSpec((GROUP, K, width), lambda g: (g, 0, 0)),
        ],
        out_shape=[out, out],
        cost_estimate=pl.CostEstimate(
            flops=2 * m_all * K * rows * width,
            transcendentals=0,
            bytes_accessed=codes_all.size * 2 + vectors.size * 2 + 2 * m_all * K * width * 2,
        ),
    )(codes_all, vectors)


def broadcast_over(x, names, count):
    copies = jnp.broadcast_to(x[None], (count,) + x.shape)
    return lax.all_to_all(copies, names, split_axis=0, concat_axis=0, tiled=True)


def shards(vectors, rotation, codes, live_rows, *, row_names, feat_names, row_sizes, order, ring):
    rows = vectors.shape[0]
    local = vectors.shape[1]
    groups = codes.shape[1]
    n_feat = rotation.shape[1] // local
    m_all = groups * n_feat
    n_row = int(np.prod(row_sizes))
    steps = steps_of(row_names, row_sizes, order)

    keep = jnp.arange(rows, dtype=jnp.int32) < live_rows[0]
    masked = jnp.where(keep[:, None], codes, -1).T
    codes_all = broadcast_over(masked.astype(jnp.bfloat16), feat_names, n_feat)
    codes_all = codes_all.reshape(m_all, rows)

    kinds = jnp.arange(K, dtype=jnp.int32)
    counts = jnp.sum(
        (masked[:, None, :] == kinds[None, :, None]).astype(jnp.float32), axis=2
    )

    h_hi, h_lo = codeword_means(codes_all, vectors)

    rot3 = rotation.reshape(local, m_all, DS).transpose(1, 0, 2)
    dims = (((2,), (1,)), ((0,), (0,)))
    partial = lax.dot_general(h_hi, rot3, dims, preferred_element_type=jnp.float32)
    partial = partial + lax.dot_general(h_lo, rot3, dims, preferred_element_type=jnp.float32)

    partial = partial.reshape(n_feat, groups, K, DS)
    sums = jnp.sum(
        lax.all_to_all(partial, feat_names, split_axis=0, concat_axis=0, tiled=True), axis=0
    )
    width = groups * DS
    packed = jnp.concatenate(
        [sums.transpose(1, 0, 2).reshape(K, width), counts.T], axis=1
    )

    if ring is None:
        packed = row_psum(packed, steps)
    else:
        ring_name, ring_size = ring
        pair_steps = [st for st in steps if st[0] != ring_name]
        packed = row_psum(packed[None], pair_steps[:1])[0]
        part = ring_scatter(packed.reshape((ring_size, K // ring_size) + packed.shape[1:]), ring_name, ring_size)
        part = row_psum(part, pair_steps[1:])
        packed = ring_gather(part, ring_name, ring_size).reshape(packed.shape)
    total_sums = packed[:, :width].reshape(K, groups, DS).transpose(1, 0, 2)
    total_counts = packed[:, width:].T
    cents = total_sums / (total_counts[:, :, None] + 1.0)
    centroids_all = cents.transpose(1, 0, 2).reshape(K, groups * DS)

    row_index = lax.axis_index(row_names)
    share = K // n_row
    centroids = lax.dynamic_slice_in_dim(centroids_all, row_index * share, share, 0)

    table = broadcast_over(cents.astype(jnp.bfloat16), feat_names, n_feat)
    table = table.reshape(m_all, K, DS)
    dims = (((1,), (1,)), ((0,), (0,)))
    grad = lax.dot_general(table, h_hi, dims, preferred_element_type=jnp.float32)
    grad = grad + lax.dot_general(table, h_lo, dims, preferred_element_type=jnp.float32)
    inverse = 1.0 / (rows * n_row)
    grad = grad.reshape(m_all * DS, local) * inverse

    grad_rows = (m_all * DS) // n_row
    pieces = grad.reshape(n_row, grad_rows, local)
    if ring is not None:
        ring_name, ring_size = ring
        pair_steps = [st for st in steps if st[0] != ring_name]
        names_sizes = list(zip(row_names, row_sizes))
        axes_order = [i for i, (n, _) in enumerate(names_sizes) if n != ring_name]
        axes_order = axes_order[::-1] + [i for i, (n, _) in enumerate(names_sizes) if n == ring_name]
        grid = pieces.reshape(tuple(sz for _, sz in names_sizes) + (grad_rows, local))
        grid = grid.transpose(tuple(axes_order) + (len(names_sizes), len(names_sizes) + 1))
        pieces = grid.reshape(n_row, grad_rows, local)
        part = row_psum_scatter(pieces, pair_steps)
        grad_t = ring_scatter(part, ring_name, ring_size)
        return centroids, grad_t
    position = []
    for r in range(n_row):
        coords = {}
        rest = r
        for name, size in reversed(list(zip(row_names, row_sizes))):
            coords[name] = rest % size
            rest //= size
        q = 0
        for name, bit, size in steps:
            q = q * 2 + ((coords[name] >> bit) & 1)
        position.append((q, r))
    source = np.array([r for _, r in sorted(position)], dtype=np.int32)
    pieces = pieces[source]
    grad_t = row_psum_scatter(pieces, steps)[0]
    return centroids, grad_t


def solution(mesh):
    row_size = mesh.shape["row"]
    feat_size = mesh.shape["feat"]
    row_sizes = tuple(s for _, s in ROW_PARTS)
    feat_sizes = tuple(s for _, s in FEAT_PARTS)
    if int(np.prod(row_sizes)) != row_size or int(np.prod(feat_sizes)) != feat_size:
        row_parts, feat_parts = (("row", row_size),), (("feat", feat_size),)
    else:
        row_parts, feat_parts = ROW_PARTS, FEAT_PARTS
    names = tuple(n for n, _ in row_parts + feat_parts)
    shape = tuple(s for _, s in row_parts + feat_parts)
    fine = Mesh(np.asarray(mesh.devices).reshape(shape), names)
    row_names = tuple(n for n, _ in row_parts)
    feat_names = tuple(n for n, _ in feat_parts)

    body = functools.partial(
        shards,
        row_names=row_names,
        feat_names=feat_names,
        row_sizes=tuple(s for _, s in row_parts),
        order=REDUCE_ORDER if row_parts is ROW_PARTS else row_names,
        ring=RING if row_parts is ROW_PARTS else None,
    )
    return jax.shard_map(
        body,
        mesh=fine,
        in_specs=(P(row_names, feat_names), P(feat_names, None), P(row_names, feat_names), P(row_names)),
        out_specs=(P(row_names, feat_names), P(row_names, feat_names)),
        check_vma=False,
    )
```

```python
import functools

import jax
import jax.numpy as jnp
import numpy as np
from jax import lax
from jax.experimental import pallas as pl
from jax.sharding import Mesh
from jax.sharding import PartitionSpec as P

K = 256
DS = 16

ROW_PARTS = (("z", 8), ("xl", 2), ("c", 2))
FEAT_PARTS = (("y", 4), ("xh", 2))
REDUCE_ORDER = ("c", "xl", "z")
GROUP = 8


def axis_bit(name, bit):
    return (lax.axis_index(name) >> bit) & 1


def steps_of(row_names, row_sizes, order):
    sizes = dict(zip(row_names, row_sizes))
    out = []
    for name in order:
        for bit in range(int(sizes[name]).bit_length() - 1):
            out.append((name, bit, sizes[name]))
    return out


def exchange(x, name, bit, size):
    pairs = [(i, i ^ (1 << bit)) for i in range(size)]
    return lax.ppermute(x, name, pairs)


def row_psum(x, steps):
    for name, bit, size in steps:
        x = x + exchange(x, name, bit, size)
    return x


def row_psum_scatter(x, steps):
    for name, bit, size in steps:
        halves = x.reshape((2, x.shape[0] // 2) + x.shape[1:])
        mine = axis_bit(name, bit)
        keep = lax.dynamic_index_in_dim(halves, mine, 0, keepdims=False)
        send = lax.dynamic_index_in_dim(halves, 1 - mine, 0, keepdims=False)
        x = keep + exchange(send, name, bit, size)
    return x


def means_kernel(codes_ref, vec_ref, rot_ref, hi_ref, lo_ref, sums_ref):
    rows = codes_ref.shape[1]
    group = codes_ref.shape[0]
    kinds = lax.broadcasted_iota(jnp.int32, (K, rows), 0).astype(codes_ref.dtype)
    one = jnp.ones((K, rows), jnp.bfloat16)
    zero = jnp.zeros((K, rows), jnp.bfloat16)
    lanes = lax.broadcasted_iota(jnp.int32, (K, group * DS), 1) // DS
    total = jnp.zeros((K, group * DS), jnp.float32)
    for i in range(group):
        hot = jnp.where(codes_ref[pl.ds(i, 1), :] == kinds, one, zero)
        h = jnp.dot(hot, vec_ref[...], preferred_element_type=jnp.float32)
        hi = h.astype(jnp.bfloat16)
        lo = (h - hi.astype(jnp.float32)).astype(jnp.bfloat16)
        hi_ref[i] = hi
        lo_ref[i] = lo
        rot = rot_ref[...]
        part = jnp.dot(hi, rot, preferred_element_type=jnp.float32)
        part = part + jnp.dot(lo, rot, preferred_element_type=jnp.float32)
        total = jnp.where(lanes == i, part, total)
    sums_ref[...] = total


def codeword_means(codes_all, vectors, rotation):
    m_all, rows = codes_all.shape
    width = vectors.shape[1]
    out = jax.ShapeDtypeStruct((m_all, K, width), jnp.bfloat16)
    sums = jax.ShapeDtypeStruct((K, m_all * DS), jnp.float32)
    return pl.pallas_call(
        means_kernel,
        grid=(m_all // GROUP,),
        in_specs=[
            pl.BlockSpec((GROUP, rows), lambda g: (g, 0)),
            pl.BlockSpec((rows, width), lambda g: (0, 0)),
            pl.BlockSpec((width, GROUP * DS), lambda g: (0, g)),
        ],
        out_specs=[
            pl.BlockSpec((GROUP, K, width), lambda g: (g, 0, 0)),
            pl.BlockSpec((GROUP, K, width), lambda g: (g, 0, 0)),
            pl.BlockSpec((K, GROUP * DS), lambda g: (0, g)),
        ],
        out_shape=[out, out, sums],
        cost_estimate=pl.CostEstimate(
            flops=2 * m_all * K * width * (rows + 2 * GROUP * DS),
            transcendentals=0,
            bytes_accessed=codes_all.size * 2
            + vectors.size * 2
            + rotation.size * 2
            + 2 * m_all * K * width * 2
            + K * m_all * DS * 4,
        ),
    )(codes_all, vectors, rotation)


def broadcast_over(x, names, count):
    copies = jnp.broadcast_to(x[None], (count,) + x.shape)
    return lax.all_to_all(copies, names, split_axis=0, concat_axis=0, tiled=True)


def shards(vectors, rotation, codes, live_rows, *, row_names, feat_names, row_sizes, order):
    rows = vectors.shape[0]
    local = vectors.shape[1]
    groups = codes.shape[1]
    n_feat = rotation.shape[1] // local
    m_all = groups * n_feat
    n_row = int(np.prod(row_sizes))
    steps = steps_of(row_names, row_sizes, order)

    keep = jnp.arange(rows, dtype=jnp.int32) < live_rows[0]
    masked = jnp.where(keep[:, None], codes, -1).T
    codes_all = broadcast_over(masked.astype(jnp.bfloat16), feat_names, n_feat)
    codes_all = codes_all.reshape(m_all, rows)

    kinds = jnp.arange(K, dtype=jnp.int32)
    counts = jnp.sum(
        (masked[:, None, :] == kinds[None, :, None]).astype(jnp.float32), axis=2
    )

    h_hi, h_lo, partial = codeword_means(codes_all, vectors, rotation)

    width = groups * DS
    partial = partial.reshape(K, n_feat, width)
    sums = jnp.sum(
        lax.all_to_all(partial, feat_names, split_axis=1, concat_axis=1, tiled=True), axis=1
    )
    packed = jnp.concatenate([sums, counts.T], axis=1)

    packed = row_psum(packed, steps)
    total_sums = packed[:, :width].reshape(K, groups, DS)
    total_counts = packed[:, width:]
    cents = total_sums / (total_counts[:, :, None] + 1.0)
    centroids_all = cents.reshape(K, width)

    row_index = lax.axis_index(row_names)
    share = K // n_row
    centroids = lax.dynamic_slice_in_dim(centroids_all, row_index * share, share, 0)

    table = broadcast_over(centroids_all.astype(jnp.bfloat16), feat_names, n_feat)
    table = table.reshape(n_feat, K, groups, DS).transpose(0, 2, 1, 3).reshape(m_all, K, DS)
    dims = (((1,), (1,)), ((0,), (0,)))
    grad = lax.dot_general(table, h_hi, dims, preferred_element_type=jnp.float32)
    grad = grad + lax.dot_general(table, h_lo, dims, preferred_element_type=jnp.float32)
    inverse = 1.0 / (rows * n_row)
    grad = grad.reshape(m_all * DS, local) * inverse

    grad_rows = (m_all * DS) // n_row
    pieces = grad.reshape(n_row, grad_rows, local)
    position = []
    for r in range(n_row):
        coords = {}
        rest = r
        for name, size in reversed(list(zip(row_names, row_sizes))):
            coords[name] = rest % size
            rest //= size
        q = 0
        for name, bit, size in steps:
            q = q * 2 + ((coords[name] >> bit) & 1)
        position.append((q, r))
    source = np.array([r for _, r in sorted(position)], dtype=np.int32)
    pieces = pieces[source]
    grad_t = row_psum_scatter(pieces, steps)[0]
    return centroids, grad_t


def solution(mesh):
    row_size = mesh.shape["row"]
    feat_size = mesh.shape["feat"]
    row_sizes = tuple(s for _, s in ROW_PARTS)
    feat_sizes = tuple(s for _, s in FEAT_PARTS)
    if int(np.prod(row_sizes)) != row_size or int(np.prod(feat_sizes)) != feat_size:
        row_parts, feat_parts = (("row", row_size),), (("feat", feat_size),)
    else:
        row_parts, feat_parts = ROW_PARTS, FEAT_PARTS
    names = tuple(n for n, _ in row_parts + feat_parts)
    shape = tuple(s for _, s in row_parts + feat_parts)
    fine = Mesh(np.asarray(mesh.devices).reshape(shape), names)
    row_names = tuple(n for n, _ in row_parts)
    feat_names = tuple(n for n, _ in feat_parts)

    body = functools.partial(
        shards,
        row_names=row_names,
        feat_names=feat_names,
        row_sizes=tuple(s for _, s in row_parts),
        order=REDUCE_ORDER if row_parts is ROW_PARTS else row_names,
    )
    return jax.shard_map(
        body,
        mesh=fine,
        in_specs=(P(row_names, feat_names), P(feat_names, None), P(row_names, feat_names), P(row_names)),
        out_specs=(P(row_names, feat_names), P(row_names, feat_names)),
        check_vma=False,
    )
```

```python
import functools

import jax
import jax.numpy as jnp
import numpy as np
from jax import lax
from jax.experimental import pallas as pl
from jax.sharding import Mesh
from jax.sharding import PartitionSpec as P

K = 256
DS = 16

ROW_PARTS = (("z", 8), ("xl", 2), ("c", 2))
FEAT_PARTS = (("y", 4), ("xh", 2))
REDUCE_ORDER = ("c", "xl", "z")
GROUP = 8


def axis_bit(name, bit):
    return (lax.axis_index(name) >> bit) & 1


def steps_of(row_names, row_sizes, order):
    sizes = dict(zip(row_names, row_sizes))
    out = []
    for name in order:
        for bit in range(int(sizes[name]).bit_length() - 1):
            out.append((name, bit, sizes[name]))
    return out


def exchange(x, name, bit, size):
    pairs = [(i, i ^ (1 << bit)) for i in range(size)]
    return lax.ppermute(x, name, pairs)


def row_psum(x, steps):
    for name, bit, size in steps:
        x = x + exchange(x, name, bit, size)
    return x


def row_psum_scatter(x, steps):
    for name, bit, size in steps:
        halves = x.reshape((2, x.shape[0] // 2) + x.shape[1:])
        mine = axis_bit(name, bit)
        keep = lax.dynamic_index_in_dim(halves, mine, 0, keepdims=False)
        send = lax.dynamic_index_in_dim(halves, 1 - mine, 0, keepdims=False)
        x = keep + exchange(send, name, bit, size)
    return x


def means_kernel(codes_ref, vec_ref, hi_ref, mid_ref, lo_ref):
    rows = codes_ref.shape[1]
    kinds = lax.broadcasted_iota(jnp.int32, (K, rows), 0).astype(codes_ref.dtype)
    one = jnp.ones((K, rows), jnp.bfloat16)
    zero = jnp.zeros((K, rows), jnp.bfloat16)
    for i in range(codes_ref.shape[0]):
        hot = jnp.where(codes_ref[pl.ds(i, 1), :] == kinds, one, zero)
        h = jnp.dot(hot, vec_ref[...], preferred_element_type=jnp.float32)
        hi = h.astype(jnp.bfloat16)
        rest = h - hi.astype(jnp.float32)
        mid = rest.astype(jnp.bfloat16)
        hi_ref[i] = hi
        mid_ref[i] = mid
        lo_ref[i] = (rest - mid.astype(jnp.float32)).astype(jnp.bfloat16)


def codeword_means(codes_all, vectors):
    m_all, rows = codes_all.shape
    width = vectors.shape[1]
    out = jax.ShapeDtypeStruct((m_all, K, width), jnp.bfloat16)
    return pl.pallas_call(
        means_kernel,
        grid=(m_all // GROUP,),
        in_specs=[
            pl.BlockSpec((GROUP, rows), lambda g: (g, 0)),
            pl.BlockSpec((rows, width), lambda g: (0, 0)),
        ],
        out_specs=[pl.BlockSpec((GROUP, K, width), lambda g: (g, 0, 0))] * 3,
        out_shape=[out] * 3,
        cost_estimate=pl.CostEstimate(
            flops=2 * m_all * K * rows * width,
            transcendentals=0,
            bytes_accessed=codes_all.size * 2 + vectors.size * 2 + 3 * m_all * K * width * 2,
        ),
    )(codes_all, vectors)


def broadcast_over(x, names, count):
    copies = jnp.broadcast_to(x[None], (count,) + x.shape)
    return lax.all_to_all(copies, names, split_axis=0, concat_axis=0, tiled=True)


def shards(vectors, rotation, codes, live_rows, *, row_names, feat_names, row_sizes, order):
    rows = vectors.shape[0]
    local = vectors.shape[1]
    groups = codes.shape[1]
    n_feat = rotation.shape[1] // local
    m_all = groups * n_feat
    n_row = int(np.prod(row_sizes))
    steps = steps_of(row_names, row_sizes, order)

    keep = jnp.arange(rows, dtype=jnp.int32) < live_rows[0]
    masked = jnp.where(keep[:, None], codes, -1).T
    codes_all = broadcast_over(masked.astype(jnp.bfloat16), feat_names, n_feat)
    codes_all = codes_all.reshape(m_all, rows)

    kinds = jnp.arange(K, dtype=jnp.int32)
    counts = jnp.sum(
        (masked[:, None, :] == kinds[None, :, None]).astype(jnp.float32), axis=2
    )

    h_parts = codeword_means(codes_all, vectors)

    rot3 = rotation.reshape(local, m_all, DS).transpose(1, 0, 2)
    dims = (((2,), (1,)), ((0,), (0,)))
    partial = sum(
        lax.dot_general(part, rot3, dims, preferred_element_type=jnp.float32) for part in h_parts
    )

    partial = partial.reshape(n_feat, groups, K, DS)
    sums = jnp.sum(
        lax.all_to_all(partial, feat_names, split_axis=0, concat_axis=0, tiled=True), axis=0
    )
    packed = jnp.concatenate([sums.reshape(groups, K * DS), counts], axis=1)

    packed = row_psum(packed, steps)
    total_sums = packed[:, : K * DS].reshape(groups, K, DS)
    total_counts = packed[:, K * DS :]
    cents = total_sums / (total_counts[:, :, None] + 1.0)
    centroids_all = cents.transpose(1, 0, 2).reshape(K, groups * DS)

    row_index = lax.axis_index(row_names)
    share = K // n_row
    centroids = lax.dynamic_slice_in_dim(centroids_all, row_index * share, share, 0)

    table = broadcast_over(cents.astype(jnp.bfloat16), feat_names, n_feat)
    table = table.reshape(m_all, K, DS)
    dims = (((1,), (1,)), ((0,), (0,)))
    grad = sum(
        lax.dot_general(table, part, dims, preferred_element_type=jnp.float32) for part in h_parts
    )
    inverse = 1.0 / (rows * n_row)
    grad = grad.reshape(m_all * DS, local) * inverse

    grad_rows = (m_all * DS) // n_row
    pieces = grad.reshape(n_row, grad_rows, local)
    position = []
    for r in range(n_row):
        coords = {}
        rest = r
        for name, size in reversed(list(zip(row_names, row_sizes))):
            coords[name] = rest % size
            rest //= size
        q = 0
        for name, bit, size in steps:
            q = q * 2 + ((coords[name] >> bit) & 1)
        position.append((q, r))
    source = np.array([r for _, r in sorted(position)], dtype=np.int32)
    pieces = pieces[source]
    grad_t = row_psum_scatter(pieces, steps)[0]
    return centroids, grad_t


def solution(mesh):
    row_size = mesh.shape["row"]
    feat_size = mesh.shape["feat"]
    row_sizes = tuple(s for _, s in ROW_PARTS)
    feat_sizes = tuple(s for _, s in FEAT_PARTS)
    if int(np.prod(row_sizes)) != row_size or int(np.prod(feat_sizes)) != feat_size:
        row_parts, feat_parts = (("row", row_size),), (("feat", feat_size),)
    else:
        row_parts, feat_parts = ROW_PARTS, FEAT_PARTS
    names = tuple(n for n, _ in row_parts + feat_parts)
    shape = tuple(s for _, s in row_parts + feat_parts)
    fine = Mesh(np.asarray(mesh.devices).reshape(shape), names)
    row_names = tuple(n for n, _ in row_parts)
    feat_names = tuple(n for n, _ in feat_parts)

    body = functools.partial(
        shards,
        row_names=row_names,
        feat_names=feat_names,
        row_sizes=tuple(s for _, s in row_parts),
        order=REDUCE_ORDER if row_parts is ROW_PARTS else row_names,
    )
    return jax.shard_map(
        body,
        mesh=fine,
        in_specs=(P(row_names, feat_names), P(feat_names, None), P(row_names, feat_names), P(row_names)),
        out_specs=(P(row_names, feat_names), P(row_names, feat_names)),
        check_vma=False,
    )
```

```python
import functools

import jax
import jax.numpy as jnp
import numpy as np
from jax import lax
from jax.experimental import pallas as pl
from jax.sharding import Mesh
from jax.sharding import PartitionSpec as P

K = 256
DS = 16

ROW_PARTS = (("z", 8), ("xl", 2), ("c", 2))
FEAT_PARTS = (("y", 4), ("xh", 2))
REDUCE_ORDER = ("c", "xl", "z")
GROUP = 8


def axis_bit(name, bit):
    return (lax.axis_index(name) >> bit) & 1


def steps_of(row_names, row_sizes, order):
    sizes = dict(zip(row_names, row_sizes))
    out = []
    for name in order:
        for bit in range(int(sizes[name]).bit_length() - 1):
            out.append((name, bit, sizes[name]))
    return out


def exchange(x, name, bit, size):
    pairs = [(i, i ^ (1 << bit)) for i in range(size)]
    return lax.ppermute(x, name, pairs)


def row_psum(x, steps):
    for name, bit, size in steps:
        x = x + exchange(x, name, bit, size)
    return x


def row_psum_scatter(x, steps):
    for name, bit, size in steps:
        halves = x.reshape((2, x.shape[0] // 2) + x.shape[1:])
        mine = axis_bit(name, bit)
        keep = lax.dynamic_index_in_dim(halves, mine, 0, keepdims=False)
        send = lax.dynamic_index_in_dim(halves, 1 - mine, 0, keepdims=False)
        x = keep + exchange(send, name, bit, size)
    return x


def means_kernel(codes_ref, vec_ref, out_ref):
    rows = codes_ref.shape[1]
    width = vec_ref.shape[1]
    kinds = lax.broadcasted_iota(jnp.int32, (K, rows), 0).astype(codes_ref.dtype)
    one = jnp.ones((K, rows), jnp.bfloat16)
    zero = jnp.zeros((K, rows), jnp.bfloat16)
    for i in range(codes_ref.shape[0]):
        hot = jnp.where(codes_ref[pl.ds(i, 1), :] == kinds, one, zero)
        h = jnp.dot(hot, vec_ref[...], preferred_element_type=jnp.float32)
        hi = h.astype(jnp.bfloat16)
        rest = h - hi.astype(jnp.float32)
        mid = rest.astype(jnp.bfloat16)
        out_ref[i, :, pl.ds(0, width)] = hi
        out_ref[i, :, pl.ds(width, width)] = mid
        out_ref[i, :, pl.ds(2 * width, width)] = (rest - mid.astype(jnp.float32)).astype(jnp.bfloat16)


def codeword_means(codes_all, vectors):
    m_all, rows = codes_all.shape
    width = vectors.shape[1]
    return pl.pallas_call(
        means_kernel,
        grid=(m_all // GROUP,),
        in_specs=[
            pl.BlockSpec((GROUP, rows), lambda g: (g, 0)),
            pl.BlockSpec((rows, width), lambda g: (0, 0)),
        ],
        out_specs=pl.BlockSpec((GROUP, K, 3 * width), lambda g: (g, 0, 0)),
        out_shape=jax.ShapeDtypeStruct((m_all, K, 3 * width), jnp.bfloat16),
        cost_estimate=pl.CostEstimate(
            flops=2 * m_all * K * rows * width,
            transcendentals=0,
            bytes_accessed=codes_all.size * 2 + vectors.size * 2 + 3 * m_all * K * width * 2,
        ),
    )(codes_all, vectors)


def broadcast_over(x, names, count):
    copies = jnp.broadcast_to(x[None], (count,) + x.shape)
    return lax.all_to_all(copies, names, split_axis=0, concat_axis=0, tiled=True)


def shards(vectors, rotation, codes, live_rows, *, row_names, feat_names, row_sizes, order):
    rows = vectors.shape[0]
    local = vectors.shape[1]
    groups = codes.shape[1]
    n_feat = rotation.shape[1] // local
    m_all = groups * n_feat
    n_row = int(np.prod(row_sizes))
    steps = steps_of(row_names, row_sizes, order)

    keep = jnp.arange(rows, dtype=jnp.int32) < live_rows[0]
    masked = jnp.where(keep[:, None], codes, -1).T
    codes_all = broadcast_over(masked.astype(jnp.bfloat16), feat_names, n_feat)
    codes_all = codes_all.reshape(m_all, rows)

    kinds = jnp.arange(K, dtype=jnp.int32)
    counts = jnp.sum(
        (masked[:, None, :] == kinds[None, :, None]).astype(jnp.float32), axis=2
    )

    h_parts = codeword_means(codes_all, vectors)

    rot3 = rotation.reshape(local, m_all, DS).transpose(1, 0, 2)
    dims = (((2,), (1,)), ((0,), (0,)))
    rot3 = jnp.concatenate([rot3] * 3, axis=1)
    partial = lax.dot_general(h_parts, rot3, dims, preferred_element_type=jnp.float32)

    partial = partial.reshape(n_feat, groups, K, DS)
    sums = jnp.sum(
        lax.all_to_all(partial, feat_names, split_axis=0, concat_axis=0, tiled=True), axis=0
    )
    packed = jnp.concatenate([sums.reshape(groups, K * DS), counts], axis=1)

    packed = row_psum(packed, steps)
    total_sums = packed[:, : K * DS].reshape(groups, K, DS)
    total_counts = packed[:, K * DS :]
    cents = total_sums / (total_counts[:, :, None] + 1.0)
    centroids_all = cents.transpose(1, 0, 2).reshape(K, groups * DS)

    row_index = lax.axis_index(row_names)
    share = K // n_row
    centroids = lax.dynamic_slice_in_dim(centroids_all, row_index * share, share, 0)

    table = broadcast_over(cents.astype(jnp.bfloat16), feat_names, n_feat)
    table = table.reshape(m_all, K, DS)
    dims = (((1,), (1,)), ((0,), (0,)))
    grad = lax.dot_general(table, h_parts, dims, preferred_element_type=jnp.float32)
    grad = grad[..., :local] + grad[..., local : 2 * local] + grad[..., 2 * local :]
    inverse = 1.0 / (rows * n_row)
    grad = grad.reshape(m_all * DS, local) * inverse

    grad_rows = (m_all * DS) // n_row
    pieces = grad.reshape(n_row, grad_rows, local)
    position = []
    for r in range(n_row):
        coords = {}
        rest = r
        for name, size in reversed(list(zip(row_names, row_sizes))):
            coords[name] = rest % size
            rest //= size
        q = 0
        for name, bit, size in steps:
            q = q * 2 + ((coords[name] >> bit) & 1)
        position.append((q, r))
    source = np.array([r for _, r in sorted(position)], dtype=np.int32)
    pieces = pieces[source]
    grad_t = row_psum_scatter(pieces, steps)[0]
    return centroids, grad_t


def solution(mesh):
    row_size = mesh.shape["row"]
    feat_size = mesh.shape["feat"]
    row_sizes = tuple(s for _, s in ROW_PARTS)
    feat_sizes = tuple(s for _, s in FEAT_PARTS)
    if int(np.prod(row_sizes)) != row_size or int(np.prod(feat_sizes)) != feat_size:
        row_parts, feat_parts = (("row", row_size),), (("feat", feat_size),)
    else:
        row_parts, feat_parts = ROW_PARTS, FEAT_PARTS
    names = tuple(n for n, _ in row_parts + feat_parts)
    shape = tuple(s for _, s in row_parts + feat_parts)
    fine = Mesh(np.asarray(mesh.devices).reshape(shape), names)
    row_names = tuple(n for n, _ in row_parts)
    feat_names = tuple(n for n, _ in feat_parts)

    body = functools.partial(
        shards,
        row_names=row_names,
        feat_names=feat_names,
        row_sizes=tuple(s for _, s in row_parts),
        order=REDUCE_ORDER if row_parts is ROW_PARTS else row_names,
    )
    return jax.shard_map(
        body,
        mesh=fine,
        in_specs=(P(row_names, feat_names), P(feat_names, None), P(row_names, feat_names), P(row_names)),
        out_specs=(P(row_names, feat_names), P(row_names, feat_names)),
        check_vma=False,
    )
```

```python
import functools

import jax
import jax.numpy as jnp
import numpy as np
from jax import lax
from jax.experimental import pallas as pl
from jax.sharding import Mesh
from jax.sharding import PartitionSpec as P

K = 256
DS = 16

ROW_PARTS = (("z", 8), ("xl", 2), ("c", 2))
FEAT_PARTS = (("y", 4), ("xh", 2))
REDUCE_ORDER = ("c", "xl", "z")
GROUP = 8


def axis_bit(name, bit):
    return (lax.axis_index(name) >> bit) & 1


def steps_of(row_names, row_sizes, order):
    sizes = dict(zip(row_names, row_sizes))
    out = []
    for name in order:
        for bit in range(int(sizes[name]).bit_length() - 1):
            out.append((name, bit, sizes[name]))
    return out


def exchange(x, name, bit, size):
    pairs = [(i, i ^ (1 << bit)) for i in range(size)]
    return lax.ppermute(x, name, pairs)


def row_psum(x, steps):
    for name, bit, size in steps:
        x = x + exchange(x, name, bit, size)
    return x


def row_psum_scatter(x, steps):
    for name, bit, size in steps:
        halves = x.reshape((2, x.shape[0] // 2) + x.shape[1:])
        mine = axis_bit(name, bit)
        keep = lax.dynamic_index_in_dim(halves, mine, 0, keepdims=False)
        send = lax.dynamic_index_in_dim(halves, 1 - mine, 0, keepdims=False)
        x = keep + exchange(send, name, bit, size)
    return x


def means_kernel(codes_ref, vec_ref, out_ref):
    rows = codes_ref.shape[1]
    width = vec_ref.shape[1]
    kinds = lax.broadcasted_iota(jnp.int32, (K, rows), 0).astype(codes_ref.dtype)
    one = jnp.ones((K, rows), jnp.bfloat16)
    zero = jnp.zeros((K, rows), jnp.bfloat16)
    for i in range(codes_ref.shape[0]):
        hot = jnp.where(codes_ref[pl.ds(i, 1), :] == kinds, one, zero)
        h = jnp.dot(hot, vec_ref[...], preferred_element_type=jnp.float32)
        hi = h.astype(jnp.bfloat16)
        rest = h - hi.astype(jnp.float32)
        mid = rest.astype(jnp.bfloat16)
        out_ref[i, :, pl.ds(0, width)] = hi
        out_ref[i, :, pl.ds(width, width)] = mid
        out_ref[i, :, pl.ds(2 * width, width)] = (rest - mid.astype(jnp.float32)).astype(jnp.bfloat16)


def codeword_means(codes_all, vectors):
    m_all, rows = codes_all.shape
    width = vectors.shape[1]
    return pl.pallas_call(
        means_kernel,
        grid=(m_all // GROUP,),
        in_specs=[
            pl.BlockSpec((GROUP, rows), lambda g: (g, 0)),
            pl.BlockSpec((rows, width), lambda g: (0, 0)),
        ],
        out_specs=pl.BlockSpec((GROUP, K, 3 * width), lambda g: (g, 0, 0)),
        out_shape=jax.ShapeDtypeStruct((m_all, K, 3 * width), jnp.bfloat16),
        cost_estimate=pl.CostEstimate(
            flops=2 * m_all * K * rows * width,
            transcendentals=0,
            bytes_accessed=codes_all.size * 2 + vectors.size * 2 + 3 * m_all * K * width * 2,
        ),
    )(codes_all, vectors)


def broadcast_over(x, names, count):
    copies = jnp.broadcast_to(x[None], (count,) + x.shape)
    return lax.all_to_all(copies, names, split_axis=0, concat_axis=0, tiled=True)


def shards(vectors, rotation, codes, live_rows, *, row_names, feat_names, row_sizes, order):
    rows = vectors.shape[0]
    local = vectors.shape[1]
    groups = codes.shape[1]
    n_feat = rotation.shape[1] // local
    m_all = groups * n_feat
    n_row = int(np.prod(row_sizes))
    steps = steps_of(row_names, row_sizes, order)

    keep = jnp.arange(rows, dtype=jnp.int32) < live_rows[0]
    masked = jnp.where(keep[:, None], codes, -1).T
    codes_all = broadcast_over(masked.astype(jnp.bfloat16), feat_names, n_feat)
    codes_all = codes_all.reshape(m_all, rows)

    kinds = jnp.arange(K, dtype=jnp.int32)
    counts = jnp.sum(
        (masked[:, None, :] == kinds[None, :, None]).astype(jnp.float32), axis=2
    )

    h_parts = codeword_means(codes_all, vectors)

    n_grp = m_all // groups
    h_grp = h_parts.reshape(n_grp, groups * K, 3 * local)
    rot_grp = rotation.reshape(local, n_grp, groups * DS).transpose(1, 0, 2)
    rot_grp = jnp.concatenate([rot_grp] * 3, axis=1)
    dims = (((2,), (1,)), ((0,), (0,)))
    blocks = lax.dot_general(h_grp, rot_grp, dims, preferred_element_type=jnp.float32)
    blocks = blocks.reshape(n_grp, groups, K, groups, DS)
    picks = jnp.arange(groups)
    partial = blocks[:, picks, :, picks, :]
    partial = partial.transpose(1, 0, 2, 3).reshape(m_all, K, DS)

    partial = partial.reshape(n_feat, groups, K, DS)
    sums = jnp.sum(
        lax.all_to_all(partial, feat_names, split_axis=0, concat_axis=0, tiled=True), axis=0
    )
    packed = jnp.concatenate([sums.reshape(groups, K * DS), counts], axis=1)

    packed = row_psum(packed, steps)
    total_sums = packed[:, : K * DS].reshape(groups, K, DS)
    total_counts = packed[:, K * DS :]
    cents = total_sums / (total_counts[:, :, None] + 1.0)
    centroids_all = cents.transpose(1, 0, 2).reshape(K, groups * DS)

    row_index = lax.axis_index(row_names)
    share = K // n_row
    centroids = lax.dynamic_slice_in_dim(centroids_all, row_index * share, share, 0)

    table = broadcast_over(cents.astype(jnp.bfloat16), feat_names, n_feat)
    table = table.reshape(n_grp, groups, K, DS)
    eye = jnp.eye(groups, dtype=jnp.bfloat16)
    table_bd = table.transpose(0, 1, 3, 2)[:, :, :, None, :] * eye[None, :, None, :, None]
    table_bd = table_bd.reshape(n_grp, groups * DS, groups * K)
    dims = (((2,), (1,)), ((0,), (0,)))
    grad = lax.dot_general(table_bd, h_grp, dims, preferred_element_type=jnp.float32)
    grad = grad[..., :local] + grad[..., local : 2 * local] + grad[..., 2 * local :]
    inverse = 1.0 / (rows * n_row)
    grad = grad.reshape(m_all * DS, local) * inverse

    grad_rows = (m_all * DS) // n_row
    pieces = grad.reshape(n_row, grad_rows, local)
    position = []
    for r in range(n_row):
        coords = {}
        rest = r
        for name, size in reversed(list(zip(row_names, row_sizes))):
            coords[name] = rest % size
            rest //= size
        q = 0
        for name, bit, size in steps:
            q = q * 2 + ((coords[name] >> bit) & 1)
        position.append((q, r))
    source = np.array([r for _, r in sorted(position)], dtype=np.int32)
    pieces = pieces[source]
    grad_t = row_psum_scatter(pieces, steps)[0]
    return centroids, grad_t


def solution(mesh):
    row_size = mesh.shape["row"]
    feat_size = mesh.shape["feat"]
    row_sizes = tuple(s for _, s in ROW_PARTS)
    feat_sizes = tuple(s for _, s in FEAT_PARTS)
    if int(np.prod(row_sizes)) != row_size or int(np.prod(feat_sizes)) != feat_size:
        row_parts, feat_parts = (("row", row_size),), (("feat", feat_size),)
    else:
        row_parts, feat_parts = ROW_PARTS, FEAT_PARTS
    names = tuple(n for n, _ in row_parts + feat_parts)
    shape = tuple(s for _, s in row_parts + feat_parts)
    fine = Mesh(np.asarray(mesh.devices).reshape(shape), names)
    row_names = tuple(n for n, _ in row_parts)
    feat_names = tuple(n for n, _ in feat_parts)

    body = functools.partial(
        shards,
        row_names=row_names,
        feat_names=feat_names,
        row_sizes=tuple(s for _, s in row_parts),
        order=REDUCE_ORDER if row_parts is ROW_PARTS else row_names,
    )
    return jax.shard_map(
        body,
        mesh=fine,
        in_specs=(P(row_names, feat_names), P(feat_names, None), P(row_names, feat_names), P(row_names)),
        out_specs=(P(row_names, feat_names), P(row_names, feat_names)),
        check_vma=False,
    )
```

```python
import functools

import jax
import jax.numpy as jnp
import numpy as np
from jax import lax
from jax.experimental import pallas as pl
from jax.sharding import Mesh
from jax.sharding import PartitionSpec as P

K = 256
DS = 16

ROW_PARTS = (("z", 8), ("xl", 2), ("c", 2))
FEAT_PARTS = (("y", 4), ("xh", 2))
REDUCE_ORDER = ("c", "xl", "z")
GROUP = 8


def axis_bit(name, bit):
    return (lax.axis_index(name) >> bit) & 1


def steps_of(row_names, row_sizes, order):
    sizes = dict(zip(row_names, row_sizes))
    out = []
    for name in order:
        for bit in range(int(sizes[name]).bit_length() - 1):
            out.append((name, bit, sizes[name]))
    return out


def exchange(x, name, bit, size):
    pairs = [(i, i ^ (1 << bit)) for i in range(size)]
    return lax.ppermute(x, name, pairs)


def pair_quad(steps):
    if len(steps) >= 2 and steps[0][2] == 2 and steps[1][2] == 2:
        return (steps[1][0], steps[0][0]), steps[2:]
    return None, steps


def quad_perm(flip):
    return [(i, i ^ flip) for i in range(4)]


def row_psum(x, steps):
    quad, steps = pair_quad(steps)
    if quad is not None:
        inner = lax.ppermute(x, quad, quad_perm(1))
        outer = lax.ppermute(x, quad, quad_perm(2))
        both = lax.ppermute(x, quad, quad_perm(3))
        x = (x + inner) + (outer + both)
    for name, bit, size in steps:
        x = x + exchange(x, name, bit, size)
    return x


def row_psum_scatter(x, steps):
    quad, steps = pair_quad(steps)
    if quad is not None:
        quarters = x.reshape((4, x.shape[0] // 4) + x.shape[1:])
        inner_bit = lax.axis_index(quad[1]) & 1
        outer_bit = lax.axis_index(quad[0]) & 1
        def quarter(i, o):
            return lax.dynamic_index_in_dim(quarters, i * 2 + o, 0, keepdims=False)
        x = quarter(inner_bit, outer_bit)
        x = x + lax.ppermute(quarter(1 - inner_bit, outer_bit), quad, quad_perm(1))
        x = x + lax.ppermute(quarter(inner_bit, 1 - outer_bit), quad, quad_perm(2))
        x = x + lax.ppermute(quarter(1 - inner_bit, 1 - outer_bit), quad, quad_perm(3))
    for name, bit, size in steps:
        halves = x.reshape((2, x.shape[0] // 2) + x.shape[1:])
        mine = axis_bit(name, bit)
        keep = lax.dynamic_index_in_dim(halves, mine, 0, keepdims=False)
        send = lax.dynamic_index_in_dim(halves, 1 - mine, 0, keepdims=False)
        x = keep + exchange(send, name, bit, size)
    return x


def means_kernel(codes_ref, vec_ref, hi_ref, mid_ref, lo_ref):
    rows = codes_ref.shape[1]
    kinds = lax.broadcasted_iota(jnp.int32, (K, rows), 0).astype(codes_ref.dtype)
    one = jnp.ones((K, rows), jnp.bfloat16)
    zero = jnp.zeros((K, rows), jnp.bfloat16)
    for i in range(codes_ref.shape[0]):
        hot = jnp.where(codes_ref[pl.ds(i, 1), :] == kinds, one, zero)
        h = jnp.dot(hot, vec_ref[...], preferred_element_type=jnp.float32)
        hi = h.astype(jnp.bfloat16)
        rest = h - hi.astype(jnp.float32)
        mid = rest.astype(jnp.bfloat16)
        hi_ref[i] = hi
        mid_ref[i] = mid
        lo_ref[i] = (rest - mid.astype(jnp.float32)).astype(jnp.bfloat16)


def codeword_means(codes_all, vectors):
    m_all, rows = codes_all.shape
    width = vectors.shape[1]
    out = jax.ShapeDtypeStruct((m_all, K, width), jnp.bfloat16)
    return pl.pallas_call(
        means_kernel,
        grid=(m_all // GROUP,),
        in_specs=[
            pl.BlockSpec((GROUP, rows), lambda g: (g, 0)),
            pl.BlockSpec((rows, width), lambda g: (0, 0)),
        ],
        out_specs=[pl.BlockSpec((GROUP, K, width), lambda g: (g, 0, 0))] * 3,
        out_shape=[out] * 3,
        cost_estimate=pl.CostEstimate(
            flops=2 * m_all * K * rows * width,
            transcendentals=0,
            bytes_accessed=codes_all.size * 2 + vectors.size * 2 + 3 * m_all * K * width * 2,
        ),
    )(codes_all, vectors)


def broadcast_over(x, names, count):
    copies = jnp.broadcast_to(x[None], (count,) + x.shape)
    return lax.all_to_all(copies, names, split_axis=0, concat_axis=0, tiled=True)


def shards(vectors, rotation, codes, live_rows, *, row_names, feat_names, row_sizes, order):
    rows = vectors.shape[0]
    local = vectors.shape[1]
    groups = codes.shape[1]
    n_feat = rotation.shape[1] // local
    m_all = groups * n_feat
    n_row = int(np.prod(row_sizes))
    steps = steps_of(row_names, row_sizes, order)

    keep = jnp.arange(rows, dtype=jnp.int32) < live_rows[0]
    masked = jnp.where(keep[:, None], codes, -1).T
    codes_all = broadcast_over(masked.astype(jnp.bfloat16), feat_names, n_feat)
    codes_all = codes_all.reshape(m_all, rows)

    kinds = jnp.arange(K, dtype=jnp.int32)
    counts = jnp.sum(
        (masked[:, None, :] == kinds[None, :, None]).astype(jnp.float32), axis=2
    )

    h_parts = codeword_means(codes_all, vectors)

    rot3 = rotation.reshape(local, m_all, DS).transpose(1, 0, 2)
    dims = (((2,), (1,)), ((0,), (0,)))
    partial = sum(
        lax.dot_general(part, rot3, dims, preferred_element_type=jnp.float32) for part in h_parts
    )

    partial = partial.reshape(n_feat, groups, K, DS)
    sums = jnp.sum(
        lax.all_to_all(partial, feat_names, split_axis=0, concat_axis=0, tiled=True), axis=0
    )
    packed = jnp.concatenate([sums.reshape(groups, K * DS), counts], axis=1)

    packed = row_psum(packed, steps)
    total_sums = packed[:, : K * DS].reshape(groups, K, DS)
    total_counts = packed[:, K * DS :]
    cents = total_sums / (total_counts[:, :, None] + 1.0)
    centroids_all = cents.transpose(1, 0, 2).reshape(K, groups * DS)

    row_index = lax.axis_index(row_names)
    share = K // n_row
    centroids = lax.dynamic_slice_in_dim(centroids_all, row_index * share, share, 0)

    table = broadcast_over(cents.astype(jnp.bfloat16), feat_names, n_feat)
    table = table.reshape(m_all, K, DS)
    dims = (((1,), (1,)), ((0,), (0,)))
    grad = sum(
        lax.dot_general(table, part, dims, preferred_element_type=jnp.float32) for part in h_parts
    )
    inverse = 1.0 / (rows * n_row)
    grad = grad.reshape(m_all * DS, local) * inverse

    grad_rows = (m_all * DS) // n_row
    pieces = grad.reshape(n_row, grad_rows, local)
    position = []
    for r in range(n_row):
        coords = {}
        rest = r
        for name, size in reversed(list(zip(row_names, row_sizes))):
            coords[name] = rest % size
            rest //= size
        q = 0
        for name, bit, size in steps:
            q = q * 2 + ((coords[name] >> bit) & 1)
        position.append((q, r))
    source = np.array([r for _, r in sorted(position)], dtype=np.int32)
    pieces = pieces[source]
    grad_t = row_psum_scatter(pieces, steps)[0]
    return centroids, grad_t


def solution(mesh):
    row_size = mesh.shape["row"]
    feat_size = mesh.shape["feat"]
    row_sizes = tuple(s for _, s in ROW_PARTS)
    feat_sizes = tuple(s for _, s in FEAT_PARTS)
    if int(np.prod(row_sizes)) != row_size or int(np.prod(feat_sizes)) != feat_size:
        row_parts, feat_parts = (("row", row_size),), (("feat", feat_size),)
    else:
        row_parts, feat_parts = ROW_PARTS, FEAT_PARTS
    names = tuple(n for n, _ in row_parts + feat_parts)
    shape = tuple(s for _, s in row_parts + feat_parts)
    fine = Mesh(np.asarray(mesh.devices).reshape(shape), names)
    row_names = tuple(n for n, _ in row_parts)
    feat_names = tuple(n for n, _ in feat_parts)

    body = functools.partial(
        shards,
        row_names=row_names,
        feat_names=feat_names,
        row_sizes=tuple(s for _, s in row_parts),
        order=REDUCE_ORDER if row_parts is ROW_PARTS else row_names,
    )
    return jax.shard_map(
        body,
        mesh=fine,
        in_specs=(P(row_names, feat_names), P(feat_names, None), P(row_names, feat_names), P(row_names)),
        out_specs=(P(row_names, feat_names), P(row_names, feat_names)),
        check_vma=False,
    )
```

```python
import functools

import jax
import jax.numpy as jnp
import numpy as np
from jax import lax
from jax.experimental import pallas as pl
from jax.experimental.pallas import tpu as pltpu
from jax.sharding import Mesh
from jax.sharding import PartitionSpec as P

K = 256
DS = 16

ROW_PARTS = (("z", 8), ("xl", 2), ("c", 2))
FEAT_PARTS = (("y", 4), ("xh", 2))
REDUCE_ORDER = ("c", "xl", "z")
GROUP = 8


def axis_bit(name, bit):
    return (lax.axis_index(name) >> bit) & 1


def steps_of(row_names, row_sizes, order):
    sizes = dict(zip(row_names, row_sizes))
    out = []
    for name in order:
        for bit in range(int(sizes[name]).bit_length() - 1):
            out.append((name, bit, sizes[name]))
    return out


def exchange(x, name, bit, size):
    pairs = [(i, i ^ (1 << bit)) for i in range(size)]
    return lax.ppermute(x, name, pairs)


def row_psum(x, steps):
    for name, bit, size in steps:
        x = x + exchange(x, name, bit, size)
    return x


def row_psum_scatter(x, steps):
    for name, bit, size in steps:
        halves = x.reshape((2, x.shape[0] // 2) + x.shape[1:])
        mine = axis_bit(name, bit)
        keep = lax.dynamic_index_in_dim(halves, mine, 0, keepdims=False)
        send = lax.dynamic_index_in_dim(halves, 1 - mine, 0, keepdims=False)
        x = keep + exchange(send, name, bit, size)
    return x


def means_kernel(block_ref, codes_ref, vec_ref, *refs):
    hi_ref, mid_ref, lo_ref = refs[-3:]
    rows = codes_ref.shape[1]
    kinds = lax.broadcasted_iota(jnp.int32, (K, rows), 0).astype(codes_ref.dtype)
    one = jnp.ones((K, rows), jnp.bfloat16)
    zero = jnp.zeros((K, rows), jnp.bfloat16)
    for i in range(codes_ref.shape[0]):
        hot = jnp.where(codes_ref[pl.ds(i, 1), :] == kinds, one, zero)
        h = jnp.dot(hot, vec_ref[...], preferred_element_type=jnp.float32)
        hi = h.astype(jnp.bfloat16)
        rest = h - hi.astype(jnp.float32)
        mid = rest.astype(jnp.bfloat16)
        hi_ref[i] = hi
        mid_ref[i] = mid
        lo_ref[i] = (rest - mid.astype(jnp.float32)).astype(jnp.bfloat16)


def codeword_means(own, codes_own, codes_all, vectors):
    m_all, rows = codes_all.shape
    width = vectors.shape[1]
    n_blocks = m_all // GROUP
    out = jax.ShapeDtypeStruct((m_all, K, width), jnp.bfloat16)
    out_block = pl.BlockSpec((GROUP, K, width), lambda g, b: (b[0], 0, 0))
    first = pl.pallas_call(
        means_kernel,
        grid_spec=pltpu.PrefetchScalarGridSpec(
            num_scalar_prefetch=1,
            grid=(1,),
            in_specs=[
                pl.BlockSpec((GROUP, rows), lambda g, b: (0, 0)),
                pl.BlockSpec((rows, width), lambda g, b: (0, 0)),
            ],
            out_specs=[out_block] * 3,
        ),
        out_shape=[out] * 3,
        cost_estimate=pl.CostEstimate(
            flops=2 * GROUP * K * rows * width,
            transcendentals=0,
            bytes_accessed=codes_own.size * 2 + vectors.size * 2 + 3 * GROUP * K * width * 2,
        ),
    )(own, codes_own, vectors)

    def other(g, b):
        return g + (g >= b[0]).astype(jnp.int32)

    rest_block = pl.BlockSpec((GROUP, K, width), lambda g, b: (other(g, b), 0, 0))
    return pl.pallas_call(
        means_kernel,
        grid_spec=pltpu.PrefetchScalarGridSpec(
            num_scalar_prefetch=1,
            grid=(n_blocks - 1,),
            in_specs=[
                pl.BlockSpec((GROUP, rows), lambda g, b: (other(g, b), 0)),
                pl.BlockSpec((rows, width), lambda g, b: (0, 0)),
                pl.BlockSpec(memory_space=pl.ANY),
                pl.BlockSpec(memory_space=pl.ANY),
                pl.BlockSpec(memory_space=pl.ANY),
            ],
            out_specs=[rest_block] * 3,
        ),
        out_shape=[out] * 3,
        input_output_aliases={3: 0, 4: 1, 5: 2},
        cost_estimate=pl.CostEstimate(
            flops=2 * (m_all - GROUP) * K * rows * width,
            transcendentals=0,
            bytes_accessed=codes_all.size * 2 + vectors.size * 2 + 3 * (m_all - GROUP) * K * width * 2,
        ),
    )(own, codes_all, vectors, *first)


def broadcast_over(x, names, count):
    copies = jnp.broadcast_to(x[None], (count,) + x.shape)
    return lax.all_to_all(copies, names, split_axis=0, concat_axis=0, tiled=True)


def shards(vectors, rotation, codes, live_rows, *, row_names, feat_names, row_sizes, order):
    rows = vectors.shape[0]
    local = vectors.shape[1]
    groups = codes.shape[1]
    n_feat = rotation.shape[1] // local
    m_all = groups * n_feat
    n_row = int(np.prod(row_sizes))
    steps = steps_of(row_names, row_sizes, order)

    keep = jnp.arange(rows, dtype=jnp.int32) < live_rows[0]
    masked = jnp.where(keep[:, None], codes, -1).T
    codes_all = broadcast_over(masked.astype(jnp.bfloat16), feat_names, n_feat)
    codes_all = codes_all.reshape(m_all, rows)

    kinds = jnp.arange(K, dtype=jnp.int32)
    counts = jnp.sum(
        (masked[:, None, :] == kinds[None, :, None]).astype(jnp.float32), axis=2
    )

    own = lax.axis_index(feat_names).reshape(1).astype(jnp.int32)
    h_parts = codeword_means(own, masked.astype(jnp.bfloat16), codes_all, vectors)

    rot3 = rotation.reshape(local, m_all, DS).transpose(1, 0, 2)
    dims = (((2,), (1,)), ((0,), (0,)))
    partial = sum(
        lax.dot_general(part, rot3, dims, preferred_element_type=jnp.float32) for part in h_parts
    )

    partial = partial.reshape(n_feat, groups, K, DS)
    sums = jnp.sum(
        lax.all_to_all(partial, feat_names, split_axis=0, concat_axis=0, tiled=True), axis=0
    )
    packed = jnp.concatenate([sums.reshape(groups, K * DS), counts], axis=1)

    packed = row_psum(packed, steps)
    total_sums = packed[:, : K * DS].reshape(groups, K, DS)
    total_counts = packed[:, K * DS :]
    cents = total_sums / (total_counts[:, :, None] + 1.0)
    centroids_all = cents.transpose(1, 0, 2).reshape(K, groups * DS)

    row_index = lax.axis_index(row_names)
    share = K // n_row
    centroids = lax.dynamic_slice_in_dim(centroids_all, row_index * share, share, 0)

    table = broadcast_over(cents.astype(jnp.bfloat16), feat_names, n_feat)
    table = table.reshape(m_all, K, DS)
    dims = (((1,), (1,)), ((0,), (0,)))
    grad = sum(
        lax.dot_general(table, part, dims, preferred_element_type=jnp.float32) for part in h_parts
    )
    inverse = 1.0 / (rows * n_row)
    grad = grad.reshape(m_all * DS, local) * inverse

    grad_rows = (m_all * DS) // n_row
    pieces = grad.reshape(n_row, grad_rows, local)
    position = []
    for r in range(n_row):
        coords = {}
        rest = r
        for name, size in reversed(list(zip(row_names, row_sizes))):
            coords[name] = rest % size
            rest //= size
        q = 0
        for name, bit, size in steps:
            q = q * 2 + ((coords[name] >> bit) & 1)
        position.append((q, r))
    source = np.array([r for _, r in sorted(position)], dtype=np.int32)
    pieces = pieces[source]
    grad_t = row_psum_scatter(pieces, steps)[0]
    return centroids, grad_t


def solution(mesh):
    row_size = mesh.shape["row"]
    feat_size = mesh.shape["feat"]
    row_sizes = tuple(s for _, s in ROW_PARTS)
    feat_sizes = tuple(s for _, s in FEAT_PARTS)
    if int(np.prod(row_sizes)) != row_size or int(np.prod(feat_sizes)) != feat_size:
        row_parts, feat_parts = (("row", row_size),), (("feat", feat_size),)
    else:
        row_parts, feat_parts = ROW_PARTS, FEAT_PARTS
    names = tuple(n for n, _ in row_parts + feat_parts)
    shape = tuple(s for _, s in row_parts + feat_parts)
    fine = Mesh(np.asarray(mesh.devices).reshape(shape), names)
    row_names = tuple(n for n, _ in row_parts)
    feat_names = tuple(n for n, _ in feat_parts)

    body = functools.partial(
        shards,
        row_names=row_names,
        feat_names=feat_names,
        row_sizes=tuple(s for _, s in row_parts),
        order=REDUCE_ORDER if row_parts is ROW_PARTS else row_names,
    )
    return jax.shard_map(
        body,
        mesh=fine,
        in_specs=(P(row_names, feat_names), P(feat_names, None), P(row_names, feat_names), P(row_names)),
        out_specs=(P(row_names, feat_names), P(row_names, feat_names)),
        check_vma=False,
    )
```

```python
import functools

import jax
import jax.numpy as jnp
import numpy as np
from jax import lax
from jax.experimental import pallas as pl
from jax.experimental.pallas import tpu as pltpu
from jax.sharding import Mesh
from jax.sharding import PartitionSpec as P

K = 256
DS = 16

ROW_PARTS = (("z", 8), ("xl", 2), ("c", 2))
FEAT_PARTS = (("y", 4), ("xh", 2))
REDUCE_ORDER = ("c", "xl", "z")
GROUP = 8


def axis_bit(name, bit):
    return (lax.axis_index(name) >> bit) & 1


def steps_of(row_names, row_sizes, order):
    sizes = dict(zip(row_names, row_sizes))
    out = []
    for name in order:
        for bit in range(int(sizes[name]).bit_length() - 1):
            out.append((name, bit, sizes[name]))
    return out


def exchange(x, name, bit, size):
    pairs = [(i, i ^ (1 << bit)) for i in range(size)]
    return lax.ppermute(x, name, pairs)


def row_psum(x, steps):
    for name, bit, size in steps:
        x = x + exchange(x, name, bit, size)
    return x


def row_psum_scatter(x, steps):
    for name, bit, size in steps:
        halves = x.reshape((2, x.shape[0] // 2) + x.shape[1:])
        mine = axis_bit(name, bit)
        keep = lax.dynamic_index_in_dim(halves, mine, 0, keepdims=False)
        send = lax.dynamic_index_in_dim(halves, 1 - mine, 0, keepdims=False)
        x = keep + exchange(send, name, bit, size)
    return x


def means_kernel(block_ref, codes_ref, vec_ref, *refs):
    hi_ref, mid_ref, lo_ref = refs[-3:]
    rows = codes_ref.shape[1]
    kinds = lax.broadcasted_iota(jnp.int32, (K, rows), 0).astype(codes_ref.dtype)
    one = jnp.ones((K, rows), jnp.bfloat16)
    zero = jnp.zeros((K, rows), jnp.bfloat16)
    for i in range(codes_ref.shape[0]):
        hot = jnp.where(codes_ref[pl.ds(i, 1), :] == kinds, one, zero)
        h = jnp.dot(hot, vec_ref[...], preferred_element_type=jnp.float32)
        hi = h.astype(jnp.bfloat16)
        rest = h - hi.astype(jnp.float32)
        mid = rest.astype(jnp.bfloat16)
        hi_ref[i] = hi
        mid_ref[i] = mid
        lo_ref[i] = (rest - mid.astype(jnp.float32)).astype(jnp.bfloat16)


def codeword_means(own, codes_own, codes_all, vectors):
    m_all, rows = codes_all.shape
    width = vectors.shape[1]
    n_blocks = m_all // GROUP
    out = jax.ShapeDtypeStruct((m_all, K, width), jnp.bfloat16)
    out_block = pl.BlockSpec((GROUP, K, width), lambda g, b: (b[0], 0, 0))
    first = pl.pallas_call(
        means_kernel,
        grid_spec=pltpu.PrefetchScalarGridSpec(
            num_scalar_prefetch=1,
            grid=(1,),
            in_specs=[
                pl.BlockSpec((GROUP, rows), lambda g, b: (0, 0)),
                pl.BlockSpec((rows, width), lambda g, b: (0, 0)),
            ],
            out_specs=[out_block] * 3,
        ),
        out_shape=[out] * 3,
        cost_estimate=pl.CostEstimate(
            flops=2 * GROUP * K * rows * width,
            transcendentals=0,
            bytes_accessed=codes_own.size * 2 + vectors.size * 2 + 3 * GROUP * K * width * 2,
        ),
    )(own, codes_own, vectors)

    def other(g, b):
        return g + (g >= b[0]).astype(jnp.int32)

    rest_block = pl.BlockSpec((GROUP, K, width), lambda g, b: (other(g, b), 0, 0))
    return pl.pallas_call(
        means_kernel,
        grid_spec=pltpu.PrefetchScalarGridSpec(
            num_scalar_prefetch=1,
            grid=(n_blocks - 1,),
            in_specs=[
                pl.BlockSpec((GROUP, rows), lambda g, b: (other(g, b), 0)),
                pl.BlockSpec((rows, width), lambda g, b: (0, 0)),
                pl.BlockSpec(memory_space=pl.ANY),
                pl.BlockSpec(memory_space=pl.ANY),
                pl.BlockSpec(memory_space=pl.ANY),
            ],
            out_specs=[rest_block] * 3,
        ),
        out_shape=[out] * 3,
        input_output_aliases={3: 0, 4: 1, 5: 2},
        cost_estimate=pl.CostEstimate(
            flops=2 * (m_all - GROUP) * K * rows * width,
            transcendentals=0,
            bytes_accessed=codes_all.size * 2 + vectors.size * 2 + 3 * (m_all - GROUP) * K * width * 2,
        ),
    )(own, codes_all, vectors, *first)


def broadcast_over(x, names, count):
    copies = jnp.broadcast_to(x[None], (count,) + x.shape)
    return lax.all_to_all(copies, names, split_axis=0, concat_axis=0, tiled=True)


def shards(vectors, rotation, codes, live_rows, *, row_names, feat_names, row_sizes, order):
    rows = vectors.shape[0]
    local = vectors.shape[1]
    groups = codes.shape[1]
    n_feat = rotation.shape[1] // local
    m_all = groups * n_feat
    n_row = int(np.prod(row_sizes))
    steps = steps_of(row_names, row_sizes, order)

    keep = jnp.arange(rows, dtype=jnp.int32) < live_rows[0]
    masked = jnp.where(keep[:, None], codes, -1).T
    codes_all = broadcast_over(masked.astype(jnp.bfloat16), feat_names, n_feat)
    codes_all = codes_all.reshape(m_all, rows)

    kinds = jnp.arange(K, dtype=jnp.int32)
    counts = jnp.sum(
        (masked[:, None, :] == kinds[None, :, None]).astype(jnp.float32), axis=2
    )

    own = lax.axis_index(feat_names).reshape(1).astype(jnp.int32)
    h_parts = codeword_means(own, masked.astype(jnp.bfloat16), codes_all, vectors)

    rot3 = rotation.reshape(local, m_all, DS).transpose(1, 0, 2)
    dims = (((2,), (1,)), ((0,), (0,)))
    partial = sum(
        lax.dot_general(part, rot3, dims, preferred_element_type=jnp.float32) for part in h_parts
    )

    partial = partial.reshape(n_feat, groups, K, DS)
    sums = jnp.sum(
        lax.all_to_all(partial, feat_names, split_axis=0, concat_axis=0, tiled=True), axis=0
    )
    packed = jnp.concatenate([sums.reshape(groups, K * DS), counts], axis=1)

    packed = row_psum(packed, steps)
    total_sums = packed[:, : K * DS].reshape(groups, K, DS)
    total_counts = packed[:, K * DS :]
    cents = total_sums / (total_counts[:, :, None] + 1.0)
    centroids_all = cents.transpose(1, 0, 2).reshape(K, groups * DS)

    row_index = lax.axis_index(row_names)
    share = K // n_row
    centroids = lax.dynamic_slice_in_dim(centroids_all, row_index * share, share, 0)

    table = broadcast_over(cents.astype(jnp.bfloat16), feat_names, n_feat)
    table = table.reshape(m_all, K, DS)
    dims = (((1,), (1,)), ((0,), (0,)))
    grad = sum(
        lax.dot_general(table, part, dims, preferred_element_type=jnp.float32) for part in h_parts
    )
    grad = grad.reshape(m_all * DS, local)

    grad_rows = (m_all * DS) // n_row
    pieces = grad.reshape(n_row, grad_rows, local)
    position = []
    for r in range(n_row):
        coords = {}
        rest = r
        for name, size in reversed(list(zip(row_names, row_sizes))):
            coords[name] = rest % size
            rest //= size
        q = 0
        for name, bit, size in steps:
            q = q * 2 + ((coords[name] >> bit) & 1)
        position.append((q, r))
    source = np.array([r for _, r in sorted(position)], dtype=np.int32)
    pieces = pieces[source]
    grad_t = row_psum_scatter(pieces, steps)[0] / float(rows * n_row)
    return centroids, grad_t


def solution(mesh):
    row_size = mesh.shape["row"]
    feat_size = mesh.shape["feat"]
    row_sizes = tuple(s for _, s in ROW_PARTS)
    feat_sizes = tuple(s for _, s in FEAT_PARTS)
    if int(np.prod(row_sizes)) != row_size or int(np.prod(feat_sizes)) != feat_size:
        row_parts, feat_parts = (("row", row_size),), (("feat", feat_size),)
    else:
        row_parts, feat_parts = ROW_PARTS, FEAT_PARTS
    names = tuple(n for n, _ in row_parts + feat_parts)
    shape = tuple(s for _, s in row_parts + feat_parts)
    fine = Mesh(np.asarray(mesh.devices).reshape(shape), names)
    row_names = tuple(n for n, _ in row_parts)
    feat_names = tuple(n for n, _ in feat_parts)

    body = functools.partial(
        shards,
        row_names=row_names,
        feat_names=feat_names,
        row_sizes=tuple(s for _, s in row_parts),
        order=REDUCE_ORDER if row_parts is ROW_PARTS else row_names,
    )
    return jax.shard_map(
        body,
        mesh=fine,
        in_specs=(P(row_names, feat_names), P(feat_names, None), P(row_names, feat_names), P(row_names)),
        out_specs=(P(row_names, feat_names), P(row_names, feat_names)),
        check_vma=False,
    )
```

```python
import functools

import jax
import jax.numpy as jnp
import numpy as np
from jax import lax
from jax.experimental import pallas as pl
from jax.experimental.pallas import tpu as pltpu
from jax.sharding import Mesh
from jax.sharding import PartitionSpec as P

K = 256
DS = 16

ROW_PARTS = (("z", 8), ("xl", 2), ("c", 2))
FEAT_PARTS = (("y", 4), ("xh", 2))
REDUCE_ORDER = ("c", "xl", "z")
GROUP = 8


def axis_bit(name, bit):
    return (lax.axis_index(name) >> bit) & 1


def steps_of(row_names, row_sizes, order):
    sizes = dict(zip(row_names, row_sizes))
    out = []
    for name in order:
        for bit in range(int(sizes[name]).bit_length() - 1):
            out.append((name, bit, sizes[name]))
    return out


def exchange(x, name, bit, size):
    pairs = [(i, i ^ (1 << bit)) for i in range(size)]
    return lax.ppermute(x, name, pairs)


def row_psum(x, steps):
    for name, bit, size in steps:
        x = x + exchange(x, name, bit, size)
    return x


def row_psum_scatter(x, steps):
    for name, bit, size in steps:
        halves = x.reshape((2, x.shape[0] // 2) + x.shape[1:])
        mine = axis_bit(name, bit)
        keep = lax.dynamic_index_in_dim(halves, mine, 0, keepdims=False)
        send = lax.dynamic_index_in_dim(halves, 1 - mine, 0, keepdims=False)
        x = keep + exchange(send, name, bit, size)
    return x


def means_kernel(block_ref, codes_ref, vec_ref, *refs):
    hi_ref, mid_ref, lo_ref = refs[-3:]
    rows = codes_ref.shape[1]
    kinds = lax.broadcasted_iota(jnp.int32, (K, rows), 0).astype(codes_ref.dtype)
    one = jnp.ones((K, rows), jnp.bfloat16)
    zero = jnp.zeros((K, rows), jnp.bfloat16)
    for i in range(codes_ref.shape[0]):
        hot = jnp.where(codes_ref[pl.ds(i, 1), :] == kinds, one, zero)
        h = jnp.dot(hot, vec_ref[...], preferred_element_type=jnp.float32)
        hi = h.astype(jnp.bfloat16)
        rest = h - hi.astype(jnp.float32)
        mid = rest.astype(jnp.bfloat16)
        hi_ref[i] = hi
        mid_ref[i] = mid
        lo_ref[i] = (rest - mid.astype(jnp.float32)).astype(jnp.bfloat16)


def codeword_means(own, codes_own, codes_all, vectors):
    m_all, rows = codes_all.shape
    width = vectors.shape[1]
    n_blocks = m_all // GROUP
    out = jax.ShapeDtypeStruct((m_all, K, width), jnp.bfloat16)
    out_block = pl.BlockSpec((GROUP, K, width), lambda g, b: (b[0], 0, 0))
    first = pl.pallas_call(
        means_kernel,
        grid_spec=pltpu.PrefetchScalarGridSpec(
            num_scalar_prefetch=1,
            grid=(1,),
            in_specs=[
                pl.BlockSpec((GROUP, rows), lambda g, b: (0, 0)),
                pl.BlockSpec((rows, width), lambda g, b: (0, 0)),
            ],
            out_specs=[out_block] * 3,
        ),
        out_shape=[out] * 3,
        cost_estimate=pl.CostEstimate(
            flops=2 * GROUP * K * rows * width,
            transcendentals=0,
            bytes_accessed=codes_own.size * 2 + vectors.size * 2 + 3 * GROUP * K * width * 2,
        ),
    )(own, codes_own, vectors)

    def other(g, b):
        return g + (g >= b[0]).astype(jnp.int32)

    rest_block = pl.BlockSpec((GROUP, K, width), lambda g, b: (other(g, b), 0, 0))
    return pl.pallas_call(
        means_kernel,
        grid_spec=pltpu.PrefetchScalarGridSpec(
            num_scalar_prefetch=1,
            grid=(n_blocks - 1,),
            in_specs=[
                pl.BlockSpec((GROUP, rows), lambda g, b: (other(g, b), 0)),
                pl.BlockSpec((rows, width), lambda g, b: (0, 0)),
                pl.BlockSpec(memory_space=pl.ANY),
                pl.BlockSpec(memory_space=pl.ANY),
                pl.BlockSpec(memory_space=pl.ANY),
            ],
            out_specs=[rest_block] * 3,
        ),
        out_shape=[out] * 3,
        input_output_aliases={3: 0, 4: 1, 5: 2},
        cost_estimate=pl.CostEstimate(
            flops=2 * (m_all - GROUP) * K * rows * width,
            transcendentals=0,
            bytes_accessed=codes_all.size * 2 + vectors.size * 2 + 3 * (m_all - GROUP) * K * width * 2,
        ),
    )(own, codes_all, vectors, *first)


def broadcast_over(x, names, count):
    copies = jnp.broadcast_to(x[None], (count,) + x.shape)
    return lax.all_to_all(copies, names, split_axis=0, concat_axis=0, tiled=True)


def shards(vectors, rotation, codes, live_rows, *, row_names, feat_names, row_sizes, order):
    rows = vectors.shape[0]
    local = vectors.shape[1]
    groups = codes.shape[1]
    n_feat = rotation.shape[1] // local
    m_all = groups * n_feat
    n_row = int(np.prod(row_sizes))
    steps = steps_of(row_names, row_sizes, order)

    keep = jnp.arange(rows, dtype=jnp.int32) < live_rows[0]
    masked = jnp.where(keep[:, None], codes, -1).T
    codes_all = broadcast_over(masked.astype(jnp.bfloat16), feat_names, n_feat)
    codes_all = codes_all.reshape(m_all, rows)

    kinds = jnp.arange(K, dtype=jnp.int32)
    counts = jnp.sum(
        (masked[:, None, :] == kinds[None, :, None]).astype(jnp.float32), axis=2
    )

    own = lax.axis_index(feat_names).reshape(1).astype(jnp.int32)
    h_parts = codeword_means(own, masked.astype(jnp.bfloat16), codes_all, vectors)

    rot3 = rotation.reshape(local, m_all, DS).transpose(1, 0, 2)
    dims = (((2,), (1,)), ((0,), (0,)))
    partial = sum(
        lax.dot_general(part, rot3, dims, preferred_element_type=jnp.float32) for part in h_parts
    )

    if "c" in row_names:
        group_names = feat_names + ("c",)
        half = K // 2
        counts = counts + lax.ppermute(counts, "c", [(0, 1), (1, 0)])
        core = lax.axis_index("c")
        counts = lax.dynamic_index_in_dim(
            counts.reshape(groups, K // 16, 2, 8), core, 2, keepdims=False
        ).reshape(groups, half)
        parts = partial.reshape(n_feat, groups, K // 16, 2, 8, DS).transpose(0, 3, 1, 2, 4, 5)
        parts = parts.reshape(2 * n_feat, groups, half, DS)
        sums = jnp.sum(
            lax.all_to_all(parts, group_names, split_axis=0, concat_axis=0, tiled=True), axis=0
        )
        packed = jnp.concatenate([sums.reshape(groups, half * DS), counts], axis=1)
        packed = row_psum(packed, [st for st in steps if st[0] != "c"])
        total_sums = packed[:, : half * DS].reshape(groups, half, DS)
        total_counts = packed[:, half * DS :]
        cents = total_sums / (total_counts[:, :, None] + 1.0)
        centroids_all = cents.transpose(1, 0, 2).reshape(half, groups * DS)
        row_index = lax.axis_index(row_names)
        share = K // n_row
        centroids = lax.dynamic_slice_in_dim(centroids_all, (row_index // 2) * share, share, 0)
        table = broadcast_over(cents.astype(jnp.bfloat16), group_names, 2 * n_feat)
        table = table.reshape(n_feat, 2, groups, K // 16, 8, DS).transpose(0, 2, 3, 1, 4, 5)
        table = table.reshape(m_all, K, DS)
    else:
        partial = partial.reshape(n_feat, groups, K, DS)
        sums = jnp.sum(
            lax.all_to_all(partial, feat_names, split_axis=0, concat_axis=0, tiled=True), axis=0
        )
        packed = jnp.concatenate([sums.reshape(groups, K * DS), counts], axis=1)
        packed = row_psum(packed, steps)
        total_sums = packed[:, : K * DS].reshape(groups, K, DS)
        total_counts = packed[:, K * DS :]
        cents = total_sums / (total_counts[:, :, None] + 1.0)
        centroids_all = cents.transpose(1, 0, 2).reshape(K, groups * DS)
        row_index = lax.axis_index(row_names)
        share = K // n_row
        centroids = lax.dynamic_slice_in_dim(centroids_all, row_index * share, share, 0)
        table = broadcast_over(cents.astype(jnp.bfloat16), feat_names, n_feat)
        table = table.reshape(m_all, K, DS)

    dims = (((1,), (1,)), ((0,), (0,)))
    grad = sum(
        lax.dot_general(table, part, dims, preferred_element_type=jnp.float32) for part in h_parts
    )
    grad = grad.reshape(m_all * DS, local)

    grad_rows = (m_all * DS) // n_row
    pieces = grad.reshape(n_row, grad_rows, local)
    position = []
    for r in range(n_row):
        coords = {}
        rest = r
        for name, size in reversed(list(zip(row_names, row_sizes))):
            coords[name] = rest % size
            rest //= size
        q = 0
        for name, bit, size in steps:
            q = q * 2 + ((coords[name] >> bit) & 1)
        position.append((q, r))
    source = np.array([r for _, r in sorted(position)], dtype=np.int32)
    pieces = pieces[source]
    grad_t = row_psum_scatter(pieces, steps)[0] / float(rows * n_row)
    return centroids, grad_t


def solution(mesh):
    row_size = mesh.shape["row"]
    feat_size = mesh.shape["feat"]
    row_sizes = tuple(s for _, s in ROW_PARTS)
    feat_sizes = tuple(s for _, s in FEAT_PARTS)
    if int(np.prod(row_sizes)) != row_size or int(np.prod(feat_sizes)) != feat_size:
        row_parts, feat_parts = (("row", row_size),), (("feat", feat_size),)
    else:
        row_parts, feat_parts = ROW_PARTS, FEAT_PARTS
    names = tuple(n for n, _ in row_parts + feat_parts)
    shape = tuple(s for _, s in row_parts + feat_parts)
    fine = Mesh(np.asarray(mesh.devices).reshape(shape), names)
    row_names = tuple(n for n, _ in row_parts)
    feat_names = tuple(n for n, _ in feat_parts)

    body = functools.partial(
        shards,
        row_names=row_names,
        feat_names=feat_names,
        row_sizes=tuple(s for _, s in row_parts),
        order=REDUCE_ORDER if row_parts is ROW_PARTS else row_names,
    )
    return jax.shard_map(
        body,
        mesh=fine,
        in_specs=(P(row_names, feat_names), P(feat_names, None), P(row_names, feat_names), P(row_names)),
        out_specs=(P(row_names, feat_names), P(row_names, feat_names)),
        check_vma=False,
    )
```

```python
import functools

import jax
import jax.numpy as jnp
import numpy as np
from jax import lax
from jax.experimental import pallas as pl
from jax.experimental.pallas import tpu as pltpu
from jax.sharding import Mesh
from jax.sharding import PartitionSpec as P

K = 256
DS = 16

ROW_PARTS = (("z", 8), ("xl", 2), ("c", 2))
FEAT_PARTS = (("y", 4), ("xh", 2))
REDUCE_ORDER = ("c", "xl", "z")
GROUP = 8


def axis_bit(name, bit):
    return (lax.axis_index(name) >> bit) & 1


def steps_of(row_names, row_sizes, order):
    sizes = dict(zip(row_names, row_sizes))
    out = []
    for name in order:
        for bit in range(int(sizes[name]).bit_length() - 1):
            out.append((name, bit, sizes[name]))
    return out


def exchange(x, name, bit, size):
    pairs = [(i, i ^ (1 << bit)) for i in range(size)]
    return lax.ppermute(x, name, pairs)


def row_psum(x, steps):
    for name, bit, size in steps:
        x = x + exchange(x, name, bit, size)
    return x


def row_psum_scatter(x, steps):
    for name, bit, size in steps:
        halves = x.reshape((2, x.shape[0] // 2) + x.shape[1:])
        mine = axis_bit(name, bit)
        keep = lax.dynamic_index_in_dim(halves, mine, 0, keepdims=False)
        send = lax.dynamic_index_in_dim(halves, 1 - mine, 0, keepdims=False)
        x = keep + exchange(send, name, bit, size)
    return x


def means_kernel(block_ref, codes_ref, vec_ref, *refs):
    hi_ref, mid_ref, lo_ref = refs[-3:]
    rows = codes_ref.shape[1]
    kinds = lax.broadcasted_iota(jnp.int32, (K, rows), 0).astype(codes_ref.dtype)
    one = jnp.ones((K, rows), jnp.bfloat16)
    zero = jnp.zeros((K, rows), jnp.bfloat16)
    for i in range(codes_ref.shape[0]):
        hot = jnp.where(codes_ref[pl.ds(i, 1), :] == kinds, one, zero)
        h = jnp.dot(hot, vec_ref[...], preferred_element_type=jnp.float32)
        hi = h.astype(jnp.bfloat16)
        rest = h - hi.astype(jnp.float32)
        mid = rest.astype(jnp.bfloat16)
        hi_ref[i] = hi
        mid_ref[i] = mid
        lo_ref[i] = (rest - mid.astype(jnp.float32)).astype(jnp.bfloat16)


def codeword_means(own, codes_own, codes_all, vectors):
    m_all, rows = codes_all.shape
    width = vectors.shape[1]
    n_blocks = m_all // GROUP
    out = jax.ShapeDtypeStruct((m_all, K, width), jnp.bfloat16)
    out_block = pl.BlockSpec((GROUP, K, width), lambda g, b: (b[0], 0, 0))
    first = pl.pallas_call(
        means_kernel,
        grid_spec=pltpu.PrefetchScalarGridSpec(
            num_scalar_prefetch=1,
            grid=(1,),
            in_specs=[
                pl.BlockSpec((GROUP, rows), lambda g, b: (0, 0)),
                pl.BlockSpec((rows, width), lambda g, b: (0, 0)),
            ],
            out_specs=[out_block] * 3,
        ),
        out_shape=[out] * 3,
        cost_estimate=pl.CostEstimate(
            flops=2 * GROUP * K * rows * width,
            transcendentals=0,
            bytes_accessed=codes_own.size * 2 + vectors.size * 2 + 3 * GROUP * K * width * 2,
        ),
    )(own, codes_own, vectors)

    def other(g, b):
        return g + (g >= b[0]).astype(jnp.int32)

    rest_block = pl.BlockSpec((GROUP, K, width), lambda g, b: (other(g, b), 0, 0))
    return pl.pallas_call(
        means_kernel,
        grid_spec=pltpu.PrefetchScalarGridSpec(
            num_scalar_prefetch=1,
            grid=(n_blocks - 1,),
            in_specs=[
                pl.BlockSpec((GROUP, rows), lambda g, b: (other(g, b), 0)),
                pl.BlockSpec((rows, width), lambda g, b: (0, 0)),
                pl.BlockSpec(memory_space=pl.ANY),
                pl.BlockSpec(memory_space=pl.ANY),
                pl.BlockSpec(memory_space=pl.ANY),
            ],
            out_specs=[rest_block] * 3,
        ),
        out_shape=[out] * 3,
        input_output_aliases={3: 0, 4: 1, 5: 2},
        cost_estimate=pl.CostEstimate(
            flops=2 * (m_all - GROUP) * K * rows * width,
            transcendentals=0,
            bytes_accessed=codes_all.size * 2 + vectors.size * 2 + 3 * (m_all - GROUP) * K * width * 2,
        ),
    )(own, codes_all, vectors, *first)


def broadcast_over(x, names, count):
    copies = jnp.broadcast_to(x[None], (count,) + x.shape)
    return lax.all_to_all(copies, names, split_axis=0, concat_axis=0, tiled=True)


def shards(vectors, rotation, codes, live_rows, *, row_names, feat_names, row_sizes, order):
    rows = vectors.shape[0]
    local = vectors.shape[1]
    groups = codes.shape[1]
    n_feat = rotation.shape[1] // local
    m_all = groups * n_feat
    n_row = int(np.prod(row_sizes))
    steps = steps_of(row_names, row_sizes, order)

    keep = jnp.arange(rows, dtype=jnp.int32) < live_rows[0]
    masked = jnp.where(keep[:, None], codes, -1).T
    codes_all = broadcast_over(masked.astype(jnp.bfloat16), feat_names, n_feat)
    codes_all = codes_all.reshape(m_all, rows)

    kinds = jnp.arange(K, dtype=jnp.int32)
    counts = jnp.sum(
        (masked[:, None, :] == kinds[None, :, None]).astype(jnp.float32), axis=2
    )

    own = lax.axis_index(feat_names).reshape(1).astype(jnp.int32)
    h_parts = codeword_means(own, masked.astype(jnp.bfloat16), codes_all, vectors)

    rot3 = rotation.reshape(local, m_all, DS).transpose(1, 0, 2)
    dims = (((2,), (1,)), ((0,), (0,)))
    partial = sum(
        lax.dot_general(part, rot3, dims, preferred_element_type=jnp.float32) for part in h_parts
    )

    if "c" in row_names:
        group_names = feat_names + ("c",)
        half = K // 2
        core = lax.axis_index("c")
        counts = counts + lax.ppermute(counts, "c", [(0, 1), (1, 0)])
        counts = lax.dynamic_index_in_dim(counts.reshape(groups, 2, half), core, 1, keepdims=False)
        parts = partial.reshape(n_feat, groups, 2, half, DS).transpose(0, 2, 1, 3, 4)
        parts = parts.reshape(2 * n_feat, groups, half, DS)
        sums = jnp.sum(
            lax.all_to_all(parts, group_names, split_axis=0, concat_axis=0, tiled=True), axis=0
        )
        packed = jnp.concatenate([sums.reshape(groups, half * DS), counts], axis=1)
        packed = row_psum(packed, [st for st in steps if st[0] != "c"])
        total_sums = packed[:, : half * DS].reshape(groups, half, DS)
        total_counts = packed[:, half * DS :]
        cents = total_sums / (total_counts[:, :, None] + 1.0)
        centroids_half = cents.transpose(1, 0, 2).reshape(half, groups * DS)
        row_index = lax.axis_index(row_names)
        share = K // n_row
        per_half = half // share
        mine = lax.dynamic_slice_in_dim(centroids_half, (row_index % per_half) * share, share, 0)
        theirs = lax.dynamic_slice_in_dim(
            centroids_half, ((row_index ^ 1) % per_half) * share, share, 0
        )
        got = lax.ppermute(theirs, "c", [(0, 1), (1, 0)])
        centroids = jnp.where(core == row_index // per_half, mine, got)
        table = broadcast_over(cents.astype(jnp.bfloat16), group_names, 2 * n_feat)
        table = table.reshape(n_feat, 2, groups, half, DS).transpose(0, 2, 1, 3, 4)
        table = table.reshape(m_all, K, DS)
    else:
        partial = partial.reshape(n_feat, groups, K, DS)
        sums = jnp.sum(
            lax.all_to_all(partial, feat_names, split_axis=0, concat_axis=0, tiled=True), axis=0
        )
        packed = jnp.concatenate([sums.reshape(groups, K * DS), counts], axis=1)
        packed = row_psum(packed, steps)
        total_sums = packed[:, : K * DS].reshape(groups, K, DS)
        total_counts = packed[:, K * DS :]
        cents = total_sums / (total_counts[:, :, None] + 1.0)
        centroids_all = cents.transpose(1, 0, 2).reshape(K, groups * DS)
        row_index = lax.axis_index(row_names)
        share = K // n_row
        centroids = lax.dynamic_slice_in_dim(centroids_all, row_index * share, share, 0)
        table = broadcast_over(cents.astype(jnp.bfloat16), feat_names, n_feat)
        table = table.reshape(m_all, K, DS)

    dims = (((1,), (1,)), ((0,), (0,)))
    grad = sum(
        lax.dot_general(table, part, dims, preferred_element_type=jnp.float32) for part in h_parts
    )
    grad = grad.reshape(m_all * DS, local)

    grad_rows = (m_all * DS) // n_row
    pieces = grad.reshape(n_row, grad_rows, local)
    position = []
    for r in range(n_row):
        coords = {}
        rest = r
        for name, size in reversed(list(zip(row_names, row_sizes))):
            coords[name] = rest % size
            rest //= size
        q = 0
        for name, bit, size in steps:
            q = q * 2 + ((coords[name] >> bit) & 1)
        position.append((q, r))
    source = np.array([r for _, r in sorted(position)], dtype=np.int32)
    pieces = pieces[source]
    grad_t = row_psum_scatter(pieces, steps)[0] / float(rows * n_row)
    return centroids, grad_t


def solution(mesh):
    row_size = mesh.shape["row"]
    feat_size = mesh.shape["feat"]
    row_sizes = tuple(s for _, s in ROW_PARTS)
    feat_sizes = tuple(s for _, s in FEAT_PARTS)
    if int(np.prod(row_sizes)) != row_size or int(np.prod(feat_sizes)) != feat_size:
        row_parts, feat_parts = (("row", row_size),), (("feat", feat_size),)
    else:
        row_parts, feat_parts = ROW_PARTS, FEAT_PARTS
    names = tuple(n for n, _ in row_parts + feat_parts)
    shape = tuple(s for _, s in row_parts + feat_parts)
    fine = Mesh(np.asarray(mesh.devices).reshape(shape), names)
    row_names = tuple(n for n, _ in row_parts)
    feat_names = tuple(n for n, _ in feat_parts)

    body = functools.partial(
        shards,
        row_names=row_names,
        feat_names=feat_names,
        row_sizes=tuple(s for _, s in row_parts),
        order=REDUCE_ORDER if row_parts is ROW_PARTS else row_names,
    )
    return jax.shard_map(
        body,
        mesh=fine,
        in_specs=(P(row_names, feat_names), P(feat_names, None), P(row_names, feat_names), P(row_names)),
        out_specs=(P(row_names, feat_names), P(row_names, feat_names)),
        check_vma=False,
    )
```

```python
import functools

import jax
import jax.numpy as jnp
import numpy as np
from jax import lax
from jax.experimental import pallas as pl
from jax.experimental.pallas import tpu as pltpu
from jax.sharding import Mesh
from jax.sharding import PartitionSpec as P

K = 256
DS = 16

ROW_PARTS = (("z", 8), ("xl", 2), ("c", 2))
FEAT_PARTS = (("y", 4), ("xh", 2))
REDUCE_ORDER = ("c", "xl", "z")
GROUP = 8


def axis_bit(name, bit):
    return (lax.axis_index(name) >> bit) & 1


def steps_of(row_names, row_sizes, order):
    sizes = dict(zip(row_names, row_sizes))
    out = []
    for name in order:
        for bit in range(int(sizes[name]).bit_length() - 1):
            out.append((name, bit, sizes[name]))
    return out


def exchange(x, name, bit, size):
    pairs = [(i, i ^ (1 << bit)) for i in range(size)]
    return lax.ppermute(x, name, pairs)


def row_psum(x, steps):
    for name, bit, size in steps:
        x = x + exchange(x, name, bit, size)
    return x


def row_psum_scatter(x, steps):
    for name, bit, size in steps:
        halves = x.reshape((2, x.shape[0] // 2) + x.shape[1:])
        mine = axis_bit(name, bit)
        keep = lax.dynamic_index_in_dim(halves, mine, 0, keepdims=False)
        send = lax.dynamic_index_in_dim(halves, 1 - mine, 0, keepdims=False)
        x = keep + exchange(send, name, bit, size)
    return x


def means_kernel(block_ref, codes_ref, vec_ref, *refs):
    hi_ref, mid_ref, lo_ref = refs[-3:]
    rows = codes_ref.shape[1]
    kinds = lax.broadcasted_iota(jnp.int32, (K, rows), 0).astype(codes_ref.dtype)
    one = jnp.ones((K, rows), jnp.bfloat16)
    zero = jnp.zeros((K, rows), jnp.bfloat16)
    for i in range(codes_ref.shape[0]):
        hot = jnp.where(codes_ref[pl.ds(i, 1), :] == kinds, one, zero)
        h = jnp.dot(hot, vec_ref[...], preferred_element_type=jnp.float32)
        hi = h.astype(jnp.bfloat16)
        rest = h - hi.astype(jnp.float32)
        mid = rest.astype(jnp.bfloat16)
        hi_ref[i] = hi
        mid_ref[i] = mid
        lo_ref[i] = (rest - mid.astype(jnp.float32)).astype(jnp.bfloat16)


def codeword_means(own, codes_own, codes_all, vectors):
    m_all, rows = codes_all.shape
    width = vectors.shape[1]
    n_blocks = m_all // GROUP
    out = jax.ShapeDtypeStruct((m_all, K, width), jnp.bfloat16)
    out_block = pl.BlockSpec((GROUP, K, width), lambda g, b: (b[0], 0, 0))
    first = pl.pallas_call(
        means_kernel,
        grid_spec=pltpu.PrefetchScalarGridSpec(
            num_scalar_prefetch=1,
            grid=(1,),
            in_specs=[
                pl.BlockSpec((GROUP, rows), lambda g, b: (0, 0)),
                pl.BlockSpec((rows, width), lambda g, b: (0, 0)),
            ],
            out_specs=[out_block] * 3,
        ),
        out_shape=[out] * 3,
        cost_estimate=pl.CostEstimate(
            flops=2 * GROUP * K * rows * width,
            transcendentals=0,
            bytes_accessed=codes_own.size * 2 + vectors.size * 2 + 3 * GROUP * K * width * 2,
        ),
    )(own, codes_own, vectors)

    def other(g, b):
        return g + (g >= b[0]).astype(jnp.int32)

    rest_block = pl.BlockSpec((GROUP, K, width), lambda g, b: (other(g, b), 0, 0))
    return pl.pallas_call(
        means_kernel,
        grid_spec=pltpu.PrefetchScalarGridSpec(
            num_scalar_prefetch=1,
            grid=(n_blocks - 1,),
            in_specs=[
                pl.BlockSpec((GROUP, rows), lambda g, b: (other(g, b), 0)),
                pl.BlockSpec((rows, width), lambda g, b: (0, 0)),
                pl.BlockSpec(memory_space=pl.ANY),
                pl.BlockSpec(memory_space=pl.ANY),
                pl.BlockSpec(memory_space=pl.ANY),
            ],
            out_specs=[rest_block] * 3,
        ),
        out_shape=[out] * 3,
        input_output_aliases={3: 0, 4: 1, 5: 2},
        cost_estimate=pl.CostEstimate(
            flops=2 * (m_all - GROUP) * K * rows * width,
            transcendentals=0,
            bytes_accessed=codes_all.size * 2 + vectors.size * 2 + 3 * (m_all - GROUP) * K * width * 2,
        ),
    )(own, codes_all, vectors, *first)


def broadcast_over(x, names, count):
    copies = jnp.broadcast_to(x[None], (count,) + x.shape)
    return lax.all_to_all(copies, names, split_axis=0, concat_axis=0, tiled=True)


def shards(vectors, rotation, codes, live_rows, *, row_names, feat_names, row_sizes, order):
    rows = vectors.shape[0]
    local = vectors.shape[1]
    groups = codes.shape[1]
    n_feat = rotation.shape[1] // local
    m_all = groups * n_feat
    n_row = int(np.prod(row_sizes))
    steps = steps_of(row_names, row_sizes, order)

    keep = jnp.arange(rows, dtype=jnp.int32) < live_rows[0]
    masked = jnp.where(keep[:, None], codes, -1).T
    codes_all = broadcast_over(masked.astype(jnp.bfloat16), feat_names, n_feat)
    codes_all = codes_all.reshape(m_all, rows)

    kinds = jnp.arange(K, dtype=jnp.int32)
    counts = jnp.sum(
        (masked[:, None, :] == kinds[None, :, None]).astype(jnp.float32), axis=2
    )

    own = lax.axis_index(feat_names).reshape(1).astype(jnp.int32)
    h_parts = codeword_means(own, masked.astype(jnp.bfloat16), codes_all, vectors)

    rot3 = rotation.reshape(local, m_all, DS).transpose(1, 0, 2)
    dims = (((2,), (1,)), ((0,), (0,)))
    partial = sum(
        lax.dot_general(part, rot3, dims, preferred_element_type=jnp.float32) for part in h_parts
    )

    if "c" in row_names:
        sub = ("xl", "c")
        group_names = feat_names + sub
        n_sub = 4
        part_k = K // n_sub
        me_sub = lax.axis_index(sub)
        def sub_perm(flip):
            return [(i, i ^ flip) for i in range(n_sub)]
        counts = sum(
            [counts] + [lax.ppermute(counts, sub, sub_perm(t)) for t in range(1, n_sub)]
        )
        counts = lax.dynamic_index_in_dim(
            counts.reshape(groups, n_sub, part_k), me_sub, 1, keepdims=False
        )
        parts = partial.reshape(n_feat, groups, n_sub, part_k, DS).transpose(0, 2, 1, 3, 4)
        parts = parts.reshape(n_sub * n_feat, groups, part_k, DS)
        sums = jnp.sum(
            lax.all_to_all(parts, group_names, split_axis=0, concat_axis=0, tiled=True), axis=0
        )
        packed = jnp.concatenate([sums.reshape(groups, part_k * DS), counts], axis=1)
        packed = row_psum(packed, [st for st in steps if st[0] not in sub])
        total_sums = packed[:, : part_k * DS].reshape(groups, part_k, DS)
        total_counts = packed[:, part_k * DS :]
        cents = total_sums / (total_counts[:, :, None] + 1.0)
        centroids_part = cents.transpose(1, 0, 2).reshape(part_k, groups * DS)
        row_index = lax.axis_index(row_names)
        share = K // n_row
        per_part = part_k // share
        base = (row_index // n_sub) % (per_part // n_sub) * n_sub
        holder = row_index // per_part
        centroids = lax.dynamic_slice_in_dim(centroids_part, (base + me_sub) * share, share, 0)
        for t in range(1, n_sub):
            theirs = lax.dynamic_slice_in_dim(
                centroids_part, (base + (me_sub ^ t)) * share, share, 0
            )
            got = lax.ppermute(theirs, sub, sub_perm(t))
            centroids = jnp.where((me_sub ^ t) == holder, got, centroids)
        table = broadcast_over(cents.astype(jnp.bfloat16), group_names, n_sub * n_feat)
        table = table.reshape(n_feat, n_sub, groups, part_k, DS).transpose(0, 2, 1, 3, 4)
        table = table.reshape(m_all, K, DS)
    else:
        partial = partial.reshape(n_feat, groups, K, DS)
        sums = jnp.sum(
            lax.all_to_all(partial, feat_names, split_axis=0, concat_axis=0, tiled=True), axis=0
        )
        packed = jnp.concatenate([sums.reshape(groups, K * DS), counts], axis=1)
        packed = row_psum(packed, steps)
        total_sums = packed[:, : K * DS].reshape(groups, K, DS)
        total_counts = packed[:, K * DS :]
        cents = total_sums / (total_counts[:, :, None] + 1.0)
        centroids_all = cents.transpose(1, 0, 2).reshape(K, groups * DS)
        row_index = lax.axis_index(row_names)
        share = K // n_row
        centroids = lax.dynamic_slice_in_dim(centroids_all, row_index * share, share, 0)
        table = broadcast_over(cents.astype(jnp.bfloat16), feat_names, n_feat)
        table = table.reshape(m_all, K, DS)

    dims = (((1,), (1,)), ((0,), (0,)))
    grad = sum(
        lax.dot_general(table, part, dims, preferred_element_type=jnp.float32) for part in h_parts
    )
    grad = grad.reshape(m_all * DS, local)

    grad_rows = (m_all * DS) // n_row
    pieces = grad.reshape(n_row, grad_rows, local)
    position = []
    for r in range(n_row):
        coords = {}
        rest = r
        for name, size in reversed(list(zip(row_names, row_sizes))):
            coords[name] = rest % size
            rest //= size
        q = 0
        for name, bit, size in steps:
            q = q * 2 + ((coords[name] >> bit) & 1)
        position.append((q, r))
    source = np.array([r for _, r in sorted(position)], dtype=np.int32)
    pieces = pieces[source]
    grad_t = row_psum_scatter(pieces, steps)[0] / float(rows * n_row)
    return centroids, grad_t


def solution(mesh):
    row_size = mesh.shape["row"]
    feat_size = mesh.shape["feat"]
    row_sizes = tuple(s for _, s in ROW_PARTS)
    feat_sizes = tuple(s for _, s in FEAT_PARTS)
    if int(np.prod(row_sizes)) != row_size or int(np.prod(feat_sizes)) != feat_size:
        row_parts, feat_parts = (("row", row_size),), (("feat", feat_size),)
    else:
        row_parts, feat_parts = ROW_PARTS, FEAT_PARTS
    names = tuple(n for n, _ in row_parts + feat_parts)
    shape = tuple(s for _, s in row_parts + feat_parts)
    fine = Mesh(np.asarray(mesh.devices).reshape(shape), names)
    row_names = tuple(n for n, _ in row_parts)
    feat_names = tuple(n for n, _ in feat_parts)

    body = functools.partial(
        shards,
        row_names=row_names,
        feat_names=feat_names,
        row_sizes=tuple(s for _, s in row_parts),
        order=REDUCE_ORDER if row_parts is ROW_PARTS else row_names,
    )
    return jax.shard_map(
        body,
        mesh=fine,
        in_specs=(P(row_names, feat_names), P(feat_names, None), P(row_names, feat_names), P(row_names)),
        out_specs=(P(row_names, feat_names), P(row_names, feat_names)),
        check_vma=False,
    )
```

```python
import functools

import jax
import jax.numpy as jnp
import numpy as np
from jax import lax
from jax.experimental import pallas as pl
from jax.experimental.pallas import tpu as pltpu
from jax.sharding import Mesh
from jax.sharding import PartitionSpec as P

K = 256
DS = 16

ROW_PARTS = (("z", 8), ("xl", 2), ("c", 2))
FEAT_PARTS = (("y", 4), ("xh", 2))
REDUCE_ORDER = ("c", "xl", "z")
GROUP = 8


def axis_bit(name, bit):
    return (lax.axis_index(name) >> bit) & 1


def steps_of(row_names, row_sizes, order):
    sizes = dict(zip(row_names, row_sizes))
    out = []
    for name in order:
        for bit in range(int(sizes[name]).bit_length() - 1):
            out.append((name, bit, sizes[name]))
    return out


def exchange(x, name, bit, size):
    pairs = [(i, i ^ (1 << bit)) for i in range(size)]
    return lax.ppermute(x, name, pairs)


def row_psum(x, steps):
    for name, bit, size in steps:
        x = x + exchange(x, name, bit, size)
    return x


def row_psum_scatter(x, steps):
    for name, bit, size in steps:
        halves = x.reshape((2, x.shape[0] // 2) + x.shape[1:])
        mine = axis_bit(name, bit)
        keep = lax.dynamic_index_in_dim(halves, mine, 0, keepdims=False)
        send = lax.dynamic_index_in_dim(halves, 1 - mine, 0, keepdims=False)
        x = keep + exchange(send, name, bit, size)
    return x


def means_kernel(block_ref, codes_ref, vec_ref, *refs):
    hi_ref, mid_ref, lo_ref = refs[-3:]
    rows = codes_ref.shape[1]
    kinds = lax.broadcasted_iota(jnp.int32, (K, rows), 0).astype(codes_ref.dtype)
    one = jnp.ones((K, rows), jnp.bfloat16)
    zero = jnp.zeros((K, rows), jnp.bfloat16)
    for i in range(codes_ref.shape[0]):
        hot = jnp.where(codes_ref[pl.ds(i, 1), :] == kinds, one, zero)
        h = jnp.dot(hot, vec_ref[...], preferred_element_type=jnp.float32)
        hi = h.astype(jnp.bfloat16)
        rest = h - hi.astype(jnp.float32)
        mid = rest.astype(jnp.bfloat16)
        hi_ref[i] = hi
        mid_ref[i] = mid
        lo_ref[i] = (rest - mid.astype(jnp.float32)).astype(jnp.bfloat16)


def codeword_means(own, codes_own, codes_all, vectors):
    m_all, rows = codes_all.shape
    width = vectors.shape[1]
    n_blocks = m_all // GROUP
    out = jax.ShapeDtypeStruct((m_all, K, width), jnp.bfloat16)
    out_block = pl.BlockSpec((GROUP, K, width), lambda g, b: (b[0], 0, 0))
    first = pl.pallas_call(
        means_kernel,
        grid_spec=pltpu.PrefetchScalarGridSpec(
            num_scalar_prefetch=1,
            grid=(1,),
            in_specs=[
                pl.BlockSpec((GROUP, rows), lambda g, b: (0, 0)),
                pl.BlockSpec((rows, width), lambda g, b: (0, 0)),
            ],
            out_specs=[out_block] * 3,
        ),
        out_shape=[out] * 3,
        cost_estimate=pl.CostEstimate(
            flops=2 * GROUP * K * rows * width,
            transcendentals=0,
            bytes_accessed=codes_own.size * 2 + vectors.size * 2 + 3 * GROUP * K * width * 2,
        ),
    )(own, codes_own, vectors)

    def other(g, b):
        return g + (g >= b[0]).astype(jnp.int32)

    rest_block = pl.BlockSpec((GROUP, K, width), lambda g, b: (other(g, b), 0, 0))
    return pl.pallas_call(
        means_kernel,
        grid_spec=pltpu.PrefetchScalarGridSpec(
            num_scalar_prefetch=1,
            grid=(n_blocks - 1,),
            in_specs=[
                pl.BlockSpec((GROUP, rows), lambda g, b: (other(g, b), 0)),
                pl.BlockSpec((rows, width), lambda g, b: (0, 0)),
                pl.BlockSpec(memory_space=pl.ANY),
                pl.BlockSpec(memory_space=pl.ANY),
                pl.BlockSpec(memory_space=pl.ANY),
            ],
            out_specs=[rest_block] * 3,
        ),
        out_shape=[out] * 3,
        input_output_aliases={3: 0, 4: 1, 5: 2},
        cost_estimate=pl.CostEstimate(
            flops=2 * (m_all - GROUP) * K * rows * width,
            transcendentals=0,
            bytes_accessed=codes_all.size * 2 + vectors.size * 2 + 3 * (m_all - GROUP) * K * width * 2,
        ),
    )(own, codes_all, vectors, *first)


def broadcast_over(x, names, count):
    copies = jnp.broadcast_to(x[None], (count,) + x.shape)
    return lax.all_to_all(copies, names, split_axis=0, concat_axis=0, tiled=True)


def shards(vectors, rotation, codes, live_rows, *, row_names, feat_names, row_sizes, order):
    rows = vectors.shape[0]
    local = vectors.shape[1]
    groups = codes.shape[1]
    n_feat = rotation.shape[1] // local
    m_all = groups * n_feat
    n_row = int(np.prod(row_sizes))
    steps = steps_of(row_names, row_sizes, order)

    keep = jnp.arange(rows, dtype=jnp.int32) < live_rows[0]
    masked = jnp.where(keep[:, None], codes, -1).T
    codes_all = broadcast_over(masked.astype(jnp.bfloat16), feat_names, n_feat)
    codes_all = codes_all.reshape(m_all, rows)

    kinds = jnp.arange(K, dtype=jnp.int32)
    counts = jnp.sum(
        (masked[:, None, :] == kinds[None, :, None]).astype(jnp.float32), axis=2
    )

    own = lax.axis_index(feat_names).reshape(1).astype(jnp.int32)
    h_parts = codeword_means(own, masked.astype(jnp.bfloat16), codes_all, vectors)

    rot3 = rotation.reshape(local, m_all, DS).transpose(1, 0, 2)
    dims = (((2,), (1,)), ((0,), (0,)))
    partial = sum(
        lax.dot_general(part, rot3, dims, preferred_element_type=jnp.float32) for part in h_parts
    )

    if "c" in row_names:
        group_names = feat_names + ("c",)
        half = K // 2
        core = lax.axis_index("c")
        counts = counts + lax.ppermute(counts, "c", [(0, 1), (1, 0)])
        counts = lax.dynamic_index_in_dim(counts.reshape(groups, 2, half), core, 1, keepdims=False)
        parts = partial.reshape(n_feat, groups, 2, half, DS).transpose(0, 2, 1, 3, 4)
        parts = parts.reshape(2 * n_feat, groups, half, DS)
        sums = jnp.sum(
            lax.all_to_all(parts, group_names, split_axis=0, concat_axis=0, tiled=True), axis=0
        )
        packed = jnp.concatenate([sums.reshape(groups, half * DS), counts], axis=1)
        packed = row_psum(packed, [st for st in steps if st[0] != "c"])
        total_sums = packed[:, : half * DS].reshape(groups, half, DS)
        total_counts = packed[:, half * DS :]
        cents = total_sums / (total_counts[:, :, None] + 1.0)
        centroids_half = cents.transpose(1, 0, 2).reshape(half, groups * DS)
        row_index = lax.axis_index(row_names)
        share = K // n_row
        per_half = half // share
        mine = lax.dynamic_slice_in_dim(centroids_half, (row_index % per_half) * share, share, 0)
        theirs = lax.dynamic_slice_in_dim(
            centroids_half, ((row_index ^ 1) % per_half) * share, share, 0
        )
        got = lax.ppermute(theirs, "c", [(0, 1), (1, 0)])
        centroids = jnp.where(core == row_index // per_half, mine, got)
        mine_half = cents.astype(jnp.bfloat16)
        other_half = lax.ppermute(mine_half, "c", [(0, 1), (1, 0)])
        low = jnp.where(core == 0, mine_half, other_half)
        high = jnp.where(core == 0, other_half, mine_half)
        table = broadcast_over(jnp.concatenate([low, high], axis=1), feat_names, n_feat)
        table = table.reshape(m_all, K, DS)
    else:
        partial = partial.reshape(n_feat, groups, K, DS)
        sums = jnp.sum(
            lax.all_to_all(partial, feat_names, split_axis=0, concat_axis=0, tiled=True), axis=0
        )
        packed = jnp.concatenate([sums.reshape(groups, K * DS), counts], axis=1)
        packed = row_psum(packed, steps)
        total_sums = packed[:, : K * DS].reshape(groups, K, DS)
        total_counts = packed[:, K * DS :]
        cents = total_sums / (total_counts[:, :, None] + 1.0)
        centroids_all = cents.transpose(1, 0, 2).reshape(K, groups * DS)
        row_index = lax.axis_index(row_names)
        share = K // n_row
        centroids = lax.dynamic_slice_in_dim(centroids_all, row_index * share, share, 0)
        table = broadcast_over(cents.astype(jnp.bfloat16), feat_names, n_feat)
        table = table.reshape(m_all, K, DS)

    dims = (((1,), (1,)), ((0,), (0,)))
    grad = sum(
        lax.dot_general(table, part, dims, preferred_element_type=jnp.float32) for part in h_parts
    )
    grad = grad.reshape(m_all * DS, local)

    grad_rows = (m_all * DS) // n_row
    pieces = grad.reshape(n_row, grad_rows, local)
    position = []
    for r in range(n_row):
        coords = {}
        rest = r
        for name, size in reversed(list(zip(row_names, row_sizes))):
            coords[name] = rest % size
            rest //= size
        q = 0
        for name, bit, size in steps:
            q = q * 2 + ((coords[name] >> bit) & 1)
        position.append((q, r))
    source = np.array([r for _, r in sorted(position)], dtype=np.int32)
    pieces = pieces[source]
    grad_t = row_psum_scatter(pieces, steps)[0] / float(rows * n_row)
    return centroids, grad_t


def solution(mesh):
    row_size = mesh.shape["row"]
    feat_size = mesh.shape["feat"]
    row_sizes = tuple(s for _, s in ROW_PARTS)
    feat_sizes = tuple(s for _, s in FEAT_PARTS)
    if int(np.prod(row_sizes)) != row_size or int(np.prod(feat_sizes)) != feat_size:
        row_parts, feat_parts = (("row", row_size),), (("feat", feat_size),)
    else:
        row_parts, feat_parts = ROW_PARTS, FEAT_PARTS
    names = tuple(n for n, _ in row_parts + feat_parts)
    shape = tuple(s for _, s in row_parts + feat_parts)
    fine = Mesh(np.asarray(mesh.devices).reshape(shape), names)
    row_names = tuple(n for n, _ in row_parts)
    feat_names = tuple(n for n, _ in feat_parts)

    body = functools.partial(
        shards,
        row_names=row_names,
        feat_names=feat_names,
        row_sizes=tuple(s for _, s in row_parts),
        order=REDUCE_ORDER if row_parts is ROW_PARTS else row_names,
    )
    return jax.shard_map(
        body,
        mesh=fine,
        in_specs=(P(row_names, feat_names), P(feat_names, None), P(row_names, feat_names), P(row_names)),
        out_specs=(P(row_names, feat_names), P(row_names, feat_names)),
        check_vma=False,
    )
```
